32 devices in a mesh: groups: 2 (over y), expert: 8 (over z, x), context: 2 (over core).
Axes of the slice: x: 2, y: 2, z: 4, core: 2. Of those that a mesh axis runs over, the one named last changes fastest.
Arguments:
- tokens: bfloat16 [2048, 3584], P(('groups', 'expert', 'context')), parts along dimension 0, may hold values from -6 to 6
- routes: int32 [2048, 8], P(('groups', 'expert', 'context')), parts along dimension 0, may hold values from 0 to 15, all different within a row; in each aligned block of 128 rows (0 to 127, 128 to 255, ...) at most 80 rows name the same one
- route_weight: float32 [2048, 8], P(('groups', 'expert', 'context')), parts along dimension 0, may hold values from 0.5 to 1.5
- w_gate: bfloat16 [8, 320, 3584], P('expert', 'context'), may hold values from -0.09375 to 0.09375
- w_up: bfloat16 [8, 320, 3584], P('expert', 'context'), may hold values from -0.09375 to 0.09375
- w_down: bfloat16 [8, 320, 3584], P('expert', 'context'), may hold values from -0.15625 to 0.15625
Outputs:
- mixed: bfloat16 [2048, 3584], P(('groups', 'expert', 'context')), parts along dimension 0
The draws below stay inside these ranges and needn't reach their ends.
There are 2 independent parts, one for each index of `groups`. The reference program is written for one: setup_inputs(seed, part) draws one part's arguments, and reference() takes and returns one part's arrays. A program takes and returns all parts, laid end to end along the dimension named above; an argument that names none is the same for every part. Nothing has to cross between parts.
Inputs may be any that keep to these rules, and one draw needn't show every extreme that they name: In each aligned block of 128 rows (the tokens of one pair of context devices) no id is named by more than 80 routes, and in some block some id is named by exactly 80. Ids of 2 and above are zero experts.
All inputs are finite; a program needn't handle non-finite values.
Results may differ from the reference program's by a relative error of at most 0.0058.
Values may be sent and summed in bfloat16 or wider, within the bound.
No kernel may reach another device: no remote copies, remote signals or barrier semaphores. Data moves between devices by JAX's collectives and lax.ppermute only.
A program may use at most 64 MiB of HBM per device.

```python
import math
import jax
import jax.numpy as jnp
import numpy as np
from jax import lax

D = 3584
HIDDEN_SIZE = 1280
TOP = 8
SHARERS = 4
TOK_DEV = 64
EXPERTS = 2
HS = 160
ROUTE_IDS = 16
CAP = 80
TOKENS = 1024
N_CONTEXT = 2


def level_of(own_key, shape, split, low, top_value):
    loudness = 1.0
    for position, shards_of in split:
        draws = jax.random.uniform(jax.random.fold_in(jax.random.fold_in(own_key, 6), position), (shards_of,), jnp.float32, low / len(split), top_value / len(split))
        loudness = loudness * jnp.repeat(jnp.exp(draws), shape[position] // shards_of).reshape((-1,) + (1,) * (len(shape) - 1 - position))
    return loudness


def assign_block(stream_key, own, number, rows, number_of, top, reach, lean):
    order = jax.random.permutation(stream_key, number_of)
    packed, common = portions_of(number_of, rows * top, reach, lean, True), portions_of(number_of, rows * top, reach, lean, False)
    places = jnp.arange(number_of)

    def named(tallies, rotation):
        used = int((tallies > 0).sum())
        fixed = max(1, used // 4)
        moved = fixed + (places - fixed + rotation * (used - fixed)) % max(1, number_of - fixed)
        return jnp.zeros((number_of,), jnp.int32).at[order[jnp.where(places < fixed, places, moved)]].set(jnp.asarray(tallies, jnp.int32))

    tallies = jnp.where(number % 4 == 0, named(packed, number // 4), named(common, number - number // 4 - 1))
    mixed = jax.random.permutation(jax.random.fold_in(own, 3), number_of)
    donor, sink = mixed[0:number_of // 2 * 2:2], mixed[1:number_of // 2 * 2:2]
    margin = jnp.minimum(tallies[donor] - 1, reach - tallies[sink]) // 2
    margin = jnp.where((donor == order[0]) | (sink == order[0]) | (tallies[sink] == 0), 0, jnp.maximum(margin, 0))
    moved = jax.random.randint(jax.random.fold_in(own, 4), (number_of // 2,), 0, 1 << 20) % (margin + 1)
    tallies = tallies.at[donor].add(-moved).at[sink].add(moved)
    items = jnp.searchsorted(jnp.cumsum(tallies), jnp.arange(rows * top), side="right").astype(jnp.int32)
    grid = items.reshape(top, rows).T
    grid = grid[jax.random.permutation(jax.random.fold_in(own, 1), rows)]
    rotation = jax.random.randint(jax.random.fold_in(own, 2), (rows, 1), 0, top)
    return jnp.take_along_axis(grid, (jnp.arange(top)[None, :] + rotation) % top, axis=1)


def portions_of(count, total, most, slope, full):
    loads = [(1 << 20) // math.isqrt(grade ** slope) + 1 for grade in range(1, count + 1)]
    largest = most if full else min(most, max(-(-total // count), total * loads[0] // sum(loads)))
    least = 1 if total - largest >= count - 1 else 0
    counts, spare = [largest] + [least] * (count - 1), total - largest - least * (count - 1)
    while spare > 0:
        candidates = [i for i in range(1, count) if counts[i] < largest] or [i for i in range(1, count) if counts[i] < most]
        mass, budget = sum([loads[i] for i in candidates]), spare
        for i in candidates:
            more = min(most - counts[i], max(1, budget * loads[i] // mass), spare)
            counts[i] = counts[i] + more
            spare = spare - more
    return np.array(counts)


def noise(key, shape, spread, most, cuts=(), kind=jnp.bfloat16):
    result = jax.random.normal(key, shape, jnp.float32) * spread
    if len(cuts) > 0:
        result = level_of(key, shape, cuts, -0.22, 0.18) * result
    return jnp.clip(result, min=-most, max=most).astype(kind)


def setup_inputs(seed: int = 0, part: int = 0) -> dict:
    key_list = jax.random.split(jax.random.key(seed), 7)
    own_keys = jax.random.split(jax.random.fold_in(key_list[6], part), 7)
    tokens = noise(own_keys[0], (TOKENS, D), 1.0, 6.0, ((0, 16),))
    routes_keys = jax.random.split(jax.random.fold_in(own_keys[1], 1), TOKENS // (2 * TOK_DEV))
    routes_turns = jax.random.permutation(jax.random.fold_in(own_keys[1], 3), TOKENS // (2 * TOK_DEV))
    routes = jax.vmap(lambda own, number: assign_block(jax.random.fold_in(own_keys[1], 2), own, number, 2 * TOK_DEV, ROUTE_IDS, TOP, CAP, 2))(routes_keys, routes_turns).reshape((TOKENS, TOP))
    route_weight = jnp.clip(0.5 + 1.0 * jax.random.uniform(own_keys[2], (TOKENS, TOP), jnp.float32) ** level_of(own_keys[2], (TOKENS, TOP), ((0, 16),), -0.2, 0.2), 0.5, 1.5)
    w_gate = noise(key_list[3], (SHARERS * EXPERTS, HIDDEN_SIZE // SHARERS, D), D ** -0.5, 0.09375, ((0, 8), (1, 2)))
    w_up = noise(key_list[4], (SHARERS * EXPERTS, HIDDEN_SIZE // SHARERS, D), D ** -0.5, 0.09375, ((0, 8), (1, 2)))
    w_down = noise(key_list[5], (SHARERS * EXPERTS, HIDDEN_SIZE // SHARERS, D), HIDDEN_SIZE ** -0.5, 0.15625, ((0, 8), (1, 2)))
    return dict(tokens=tokens, routes=routes, route_weight=route_weight, w_gate=w_gate, w_up=w_up, w_down=w_down)


def reference(tokens, routes, route_weight, w_gate, w_up, w_down):
    blocks = TOKENS // (2 * TOK_DEV)
    per_block = 2 * TOK_DEV * TOP
    flat = routes.reshape(blocks, per_block)
    onehot = (flat[:, :, None] == jnp.arange(EXPERTS, dtype=jnp.int32)[None, None, :]).astype(jnp.int32)
    earlier = jnp.cumsum(onehot, axis=1) - onehot
    slot = jnp.sum(earlier * onehot, axis=2).astype(jnp.int32)
    real = flat < EXPERTS
    block_ids = jnp.arange(blocks, dtype=jnp.int32)[:, None]
    cells = EXPERTS * blocks * CAP
    target = jnp.where(real, (flat * blocks + block_ids) * CAP + slot, cells).astype(jnp.int32).reshape(-1)
    source = (block_ids * (2 * TOK_DEV) + jnp.arange(per_block, dtype=jnp.int32)[None, :] // TOP).astype(jnp.int32).reshape(-1)
    src_of_cell = jnp.zeros((cells,), jnp.int32).at[target].set(source, mode="drop")
    live = jnp.zeros((cells,), jnp.float32).at[target].set(1.0, mode="drop")
    weight_of_cell = jnp.zeros((cells,), jnp.float32).at[target].set(route_weight.reshape(-1), mode="drop")
    buffer = tokens[src_of_cell].reshape(EXPERTS, blocks * CAP, D)
    gate_all = w_gate.reshape(EXPERTS, HIDDEN_SIZE, D)
    up_all = w_up.reshape(EXPERTS, HIDDEN_SIZE, D)
    down_all = w_down.reshape(EXPERTS, SHARERS, N_CONTEXT, HS, D)
    dims = (((1,), (1,)), ((), ()))

    def one_expert(items):
        rows, wg, wu, wd = items
        gate = lax.dot_general(rows, wg, dims, preferred_element_type=jnp.float32)
        up = lax.dot_general(rows, wu, dims, preferred_element_type=jnp.float32)
        hidden = (jax.nn.silu(gate) * up).astype(jnp.bfloat16)
        slabs = hidden.reshape(rows.shape[0], SHARERS, N_CONTEXT, HS).astype(jnp.float32)
        parts = jnp.einsum("rqcj,qcjd->rqcd", slabs, wd.astype(jnp.float32))
        parts = lax.optimization_barrier(parts.astype(jnp.bfloat16))
        return jnp.sum(parts.astype(jnp.float32), axis=(1, 2))

    outputs = lax.map(one_expert, (buffer, gate_all, up_all, down_all)).reshape(cells, D)
    scaled = outputs * (weight_of_cell * live)[:, None]
    mixed = jnp.zeros((TOKENS, D), jnp.float32).at[src_of_cell].add(scaled)
    return mixed.astype(jnp.bfloat16)
```

```python
import jax
import jax.numpy as jnp
from jax import lax
from jax.sharding import Mesh
from jax.sharding import PartitionSpec as P

SHARERS = 4
RETURN_DTYPE = jnp.float32


def expert_rows(rows, w_gate, w_up, w_down):
    dims = (((1,), (1,)), ((), ()))
    gate = lax.dot_general(rows, w_gate[0], dims, preferred_element_type=jnp.float32)
    up = lax.dot_general(rows, w_up[0], dims, preferred_element_type=jnp.float32)
    hidden = (jax.nn.silu(gate) * up).astype(jnp.bfloat16)
    return jnp.dot(hidden, w_down[0], preferred_element_type=jnp.float32).astype(jnp.bfloat16)


def per_device(tokens, routes, route_weight, w_gate, w_up, w_down):
    tok = tokens.shape[0]
    top = routes.shape[1]
    width = tokens.shape[1]
    experts = lax.axis_size("ex")
    sharers = lax.axis_size("sh")
    n_ctx = lax.axis_size("context")
    route_count = max(5 * experts, 2 * top)
    capacity = max(2, 5 * tok * top // (2 * route_count))
    half = -(-capacity // n_ctx)
    span = n_ctx * half
    ctx = lax.axis_index("context")

    pair_routes = lax.all_gather(routes, "context", axis=0, tiled=True)
    flat = pair_routes.reshape(-1)
    onehot = (flat[:, None] == jnp.arange(experts, dtype=jnp.int32)[None, :]).astype(jnp.int32)
    earlier = jnp.cumsum(onehot, axis=0) - onehot
    slot = jnp.sum(earlier * onehot, axis=1)
    real = flat < experts
    cell = jnp.where(real, flat * span + slot, experts * span)
    pair_cell = cell.reshape(n_ctx * tok, top)

    own_cells = (
        jnp.arange(experts, dtype=jnp.int32)[:, None] * span
        + ctx * half
        + jnp.arange(half, dtype=jnp.int32)[None, :]
    ).reshape(-1)
    match = pair_cell[None, :, :] == own_cells[:, None, None]
    picker = jnp.sum(match.astype(jnp.float32), axis=2).astype(jnp.bfloat16)
    pair_tokens = lax.all_gather(tokens, "context", axis=0, tiled=True)
    packed = jnp.dot(picker, pair_tokens, preferred_element_type=jnp.float32).astype(jnp.bfloat16)
    packed = packed.reshape(experts, half, width)

    sent = lax.all_to_all(packed, "ex", split_axis=0, concat_axis=0, tiled=True)
    group_rows = lax.all_gather(sent, "sh", axis=0, tiled=False)
    all_rows = lax.all_gather(group_rows, "context", axis=0, tiled=False)
    partial = expert_rows(all_rows.reshape(-1, width), w_gate, w_up, w_down)
    partial = partial.reshape(n_ctx, sharers, experts, half, width)

    chip_parts = lax.all_to_all(partial, "context", split_axis=0, concat_axis=0, tiled=True)
    chip_sum = jnp.sum(chip_parts.astype(jnp.float32), axis=0).astype(jnp.bfloat16)
    group_parts = lax.all_to_all(chip_sum, "sh", split_axis=0, concat_axis=0, tiled=True)
    expert_out = jnp.sum(group_parts.astype(jnp.float32), axis=0).astype(RETURN_DTYPE)
    back = lax.all_to_all(expert_out, "ex", split_axis=0, concat_axis=0, tiled=True)
    slots_out = lax.all_gather(back, "context", axis=0, tiled=False).astype(jnp.float32)
    slots_out = slots_out.reshape(n_ctx * experts * half, width)

    own_cell = lax.dynamic_slice_in_dim(pair_cell, ctx * tok, tok, axis=0)
    expert_of = own_cell // span
    slot_of = own_cell % span
    layout = (slot_of // half) * (experts * half) + expert_of * half + slot_of % half
    layout = jnp.where(own_cell < experts * span, layout, n_ctx * experts * half)
    own_match = (
        layout[:, :, None] == jnp.arange(n_ctx * experts * half, dtype=jnp.int32)[None, None, :]
    ).astype(jnp.float32)
    mixing = jnp.sum(own_match * route_weight[:, :, None], axis=1)
    mixed = jnp.dot(
        mixing, slots_out, precision=lax.Precision.HIGHEST, preferred_element_type=jnp.float32
    )
    return mixed.astype(jnp.bfloat16)


def solution(mesh):
    groups, n_expert, n_ctx = mesh.devices.shape
    split = Mesh(
        mesh.devices.reshape(groups, n_expert // SHARERS, SHARERS, n_ctx),
        ("groups", "ex", "sh", "context"),
    )
    rows = P(("groups", "ex", "sh", "context"), None)
    slabs = P(("ex", "sh"), "context", None)
    return jax.shard_map(
        per_device,
        mesh=split,
        in_specs=(rows, rows, rows, slabs, slabs, slabs),
        out_specs=rows,
        check_vma=False,
    )
```

```python
import jax
import jax.numpy as jnp
from jax import lax
from jax.sharding import Mesh
from jax.sharding import PartitionSpec as P

SHARERS = 4
RETURN_DTYPE = jnp.bfloat16


def shift(x, axis, size, k):
    return lax.ppermute(x, axis, [(i, (i + k) % size) for i in range(size)])


def quarter_rows(rows, w_gate, w_up, w_down, n_ctx):
    dims = (((1,), (1,)), ((), ()))
    gate = lax.dot_general(rows, w_gate, dims, preferred_element_type=jnp.float32)
    up = lax.dot_general(rows, w_up, dims, preferred_element_type=jnp.float32)
    hidden = (jax.nn.silu(gate) * up).astype(jnp.bfloat16)
    slab = w_down.shape[0] // n_ctx
    total = None
    for c in range(n_ctx):
        part = jnp.dot(
            hidden[:, c * slab : (c + 1) * slab],
            w_down[c * slab : (c + 1) * slab],
            preferred_element_type=jnp.float32,
        ).astype(jnp.bfloat16)
        total = part.astype(jnp.float32) if total is None else total + part.astype(jnp.float32)
    return total


def per_device(tokens, routes, route_weight, w_gate, w_up, w_down):
    tok = tokens.shape[0]
    top = routes.shape[1]
    width = tokens.shape[1]
    experts = lax.axis_size("ex")
    sharers = lax.axis_size("sh")
    n_ctx = lax.axis_size("context")
    route_count = max(5 * experts, 2 * top)
    capacity = max(2, 5 * tok * top // (2 * route_count))
    half = -(-capacity // n_ctx)
    span = n_ctx * half
    ctx = lax.axis_index("context")
    me = lax.axis_index("ex")
    mine = lax.axis_index("sh")

    wg = lax.all_gather(w_gate[0], "context", axis=0, tiled=True)
    wu = lax.all_gather(w_up[0], "context", axis=0, tiled=True)
    wd = lax.all_gather(w_down[0], "context", axis=0, tiled=True)

    pair_routes = lax.all_gather(routes, "context", axis=0, tiled=True)
    flat = pair_routes.reshape(-1)
    onehot = (flat[:, None] == jnp.arange(experts, dtype=jnp.int32)[None, :]).astype(jnp.int32)
    earlier = jnp.cumsum(onehot, axis=0) - onehot
    slot = jnp.sum(earlier * onehot, axis=1)
    real = flat < experts
    cell = jnp.where(real, flat * span + slot, experts * span)
    pair_cell = cell.reshape(n_ctx * tok, top)

    if experts == 2:
        expert_order = jnp.stack([me, 1 - me])
    else:
        expert_order = jnp.arange(experts, dtype=jnp.int32)
    own_cells = (
        expert_order[:, None] * span + ctx * half + jnp.arange(half, dtype=jnp.int32)[None, :]
    ).reshape(-1)
    match = pair_cell[None, :, :] == own_cells[:, None, None]
    picker = jnp.sum(match.astype(jnp.float32), axis=2).astype(jnp.bfloat16)
    pair_tokens = lax.all_gather(tokens, "context", axis=0, tiled=True)
    packed = jnp.dot(picker, pair_tokens, preferred_element_type=jnp.float32).astype(jnp.bfloat16)
    packed = packed.reshape(experts, half, width)

    if experts == 2:
        sent = jnp.stack([packed[0], shift(packed[1], "ex", 2, 1)])
    else:
        sent = lax.all_to_all(packed, "ex", split_axis=0, concat_axis=0, tiled=True)
    group = [sent] + [shift(sent, "sh", sharers, k) for k in range(1, sharers)]
    rows = jnp.stack(group).reshape(-1, width)
    partial = quarter_rows(rows, wg, wu, wd, n_ctx).astype(jnp.bfloat16)
    partial = partial.reshape(sharers, experts, half, width)

    total = partial[0].astype(jnp.float32)
    for k in range(1, sharers):
        total = total + shift(partial[k], "sh", sharers, -k).astype(jnp.float32)
    expert_out = total.astype(RETURN_DTYPE)
    if experts == 2:
        back = jnp.stack([expert_out[0], shift(expert_out[1], "ex", 2, 1)])
    else:
        back = lax.all_to_all(expert_out, "ex", split_axis=0, concat_axis=0, tiled=True)
    slots_out = lax.all_gather(back, "context", axis=0, tiled=False).astype(jnp.float32)
    slots_out = slots_out.reshape(n_ctx * experts * half, width)

    own_cell = lax.dynamic_slice_in_dim(pair_cell, ctx * tok, tok, axis=0)
    expert_of = own_cell // span
    slot_of = own_cell % span
    if experts == 2:
        position = jnp.where(expert_of == me, 0, 1)
    else:
        position = expert_of
    layout = (slot_of // half) * (experts * half) + position * half + slot_of % half
    layout = jnp.where(own_cell < experts * span, layout, n_ctx * experts * half)
    own_match = (
        layout[:, :, None] == jnp.arange(n_ctx * experts * half, dtype=jnp.int32)[None, None, :]
    ).astype(jnp.float32)
    mixing = jnp.sum(own_match * route_weight[:, :, None], axis=1)
    mixed = jnp.dot(
        mixing, slots_out, precision=lax.Precision.HIGHEST, preferred_element_type=jnp.float32
    )
    return mixed.astype(jnp.bfloat16)


def solution(mesh):
    groups, n_expert, n_ctx = mesh.devices.shape
    split = Mesh(
        mesh.devices.reshape(groups, n_expert // SHARERS, SHARERS, n_ctx),
        ("groups", "ex", "sh", "context"),
    )
    rows = P(("groups", "ex", "sh", "context"), None)
    slabs = P(("ex", "sh"), "context", None)
    return jax.shard_map(
        per_device,
        mesh=split,
        in_specs=(rows, rows, rows, slabs, slabs, slabs),
        out_specs=rows,
        check_vma=False,
    )
```

```python
import jax
import jax.numpy as jnp
from jax import lax
from jax.sharding import Mesh
from jax.sharding import PartitionSpec as P

SHARERS = 4
RETURN_DTYPE = jnp.bfloat16


def shift(x, axis, size, k):
    return lax.ppermute(x, axis, [(i, (i + k) % size) for i in range(size)])


def quarter_rows(rows, w_gate, w_up, w_down, n_ctx):
    dims = (((1,), (1,)), ((), ()))
    gate = lax.dot_general(rows, w_gate, dims, preferred_element_type=jnp.float32)
    up = lax.dot_general(rows, w_up, dims, preferred_element_type=jnp.float32)
    hidden = (jax.nn.silu(gate) * up).astype(jnp.bfloat16)
    slab = w_down.shape[0] // n_ctx
    total = None
    for c in range(n_ctx):
        part = jnp.dot(
            hidden[:, c * slab : (c + 1) * slab],
            w_down[c * slab : (c + 1) * slab],
            preferred_element_type=jnp.float32,
        ).astype(jnp.bfloat16)
        total = part.astype(jnp.float32) if total is None else total + part.astype(jnp.float32)
    return total


def per_device(tokens, routes, route_weight, w_gate, w_up, w_down):
    tok = tokens.shape[0]
    top = routes.shape[1]
    width = tokens.shape[1]
    experts = lax.axis_size("ex")
    sharers = lax.axis_size("sh")
    n_ctx = lax.axis_size("context")
    route_count = max(5 * experts, 2 * top)
    capacity = max(2, 5 * tok * top // (2 * route_count))
    half = -(-capacity // n_ctx)
    span = n_ctx * half
    ctx = lax.axis_index("context")
    me = lax.axis_index("ex")

    wg = lax.all_gather(w_gate[0], "context", axis=0, tiled=True)
    wu = lax.all_gather(w_up[0], "context", axis=0, tiled=True)
    wd = lax.all_gather(w_down[0], "context", axis=0, tiled=True)

    pair_routes = lax.all_gather(routes, "context", axis=0, tiled=True)
    flat = pair_routes.reshape(-1)
    onehot = (flat[:, None] == jnp.arange(experts, dtype=jnp.int32)[None, :]).astype(jnp.int32)
    earlier = jnp.cumsum(onehot, axis=0) - onehot
    slot = jnp.sum(earlier * onehot, axis=1)
    real = flat < experts
    cell = jnp.where(real, flat * span + slot, experts * span)
    pair_cell = cell.reshape(n_ctx * tok, top)

    if experts == 2:
        expert_order = jnp.stack([me, 1 - me])
    else:
        expert_order = jnp.arange(experts, dtype=jnp.int32)
    own_cells = (
        expert_order[:, None] * span + ctx * half + jnp.arange(half, dtype=jnp.int32)[None, :]
    ).reshape(-1)
    match = pair_cell[None, :, :] == own_cells[:, None, None]
    picker = jnp.sum(match.astype(jnp.float32), axis=2).astype(jnp.bfloat16)
    pair_tokens = lax.all_gather(tokens, "context", axis=0, tiled=True)
    packed = jnp.dot(picker, pair_tokens, preferred_element_type=jnp.float32).astype(jnp.bfloat16)
    packed = packed.reshape(experts, half, width)

    def through_group(sent):
        group = [sent] + [shift(sent, "sh", sharers, k) for k in range(1, sharers)]
        rows = jnp.stack(group).reshape(-1, width)
        partial = quarter_rows(rows, wg, wu, wd, n_ctx).astype(jnp.bfloat16)
        partial = partial.reshape((sharers,) + sent.shape)
        total = partial[0].astype(jnp.float32)
        for k in range(1, sharers):
            total = total + shift(partial[k], "sh", sharers, -k).astype(jnp.float32)
        return total

    if experts == 2:
        local_out = through_group(packed[0:1])
        far_out = through_group(shift(packed[1:2], "ex", 2, 1))
        back = shift(far_out.astype(RETURN_DTYPE), "ex", 2, 1).astype(jnp.float32)
        mine = jnp.concatenate([local_out, back], axis=0)
    else:
        sent = lax.all_to_all(packed, "ex", split_axis=0, concat_axis=0, tiled=True)
        expert_out = through_group(sent).astype(RETURN_DTYPE)
        mine = lax.all_to_all(expert_out, "ex", split_axis=0, concat_axis=0, tiled=True)
        mine = mine.astype(jnp.float32)
    theirs = shift(mine, "context", n_ctx, 1)
    slots_out = jnp.concatenate([mine, theirs], axis=0).reshape(n_ctx * experts * half, width)

    own_cell = lax.dynamic_slice_in_dim(pair_cell, ctx * tok, tok, axis=0)
    expert_of = own_cell // span
    slot_of = own_cell % span
    if experts == 2:
        position = jnp.where(expert_of == me, 0, 1)
    else:
        position = expert_of
    block = jnp.where(slot_of // half == ctx, 0, 1)
    layout = block * (experts * half) + position * half + slot_of % half
    layout = jnp.where(own_cell < experts * span, layout, n_ctx * experts * half)
    own_match = (
        layout[:, :, None] == jnp.arange(n_ctx * experts * half, dtype=jnp.int32)[None, None, :]
    ).astype(jnp.float32)
    mixing = jnp.sum(own_match * route_weight[:, :, None], axis=1)
    mixed = jnp.dot(
        mixing, slots_out, precision=lax.Precision.HIGHEST, preferred_element_type=jnp.float32
    )
    return mixed.astype(jnp.bfloat16)


def solution(mesh):
    groups, n_expert, n_ctx = mesh.devices.shape
    split = Mesh(
        mesh.devices.reshape(groups, n_expert // SHARERS, SHARERS, n_ctx),
        ("groups", "ex", "sh", "context"),
    )
    rows = P(("groups", "ex", "sh", "context"), None)
    slabs = P(("ex", "sh"), "context", None)
    return jax.shard_map(
        per_device,
        mesh=split,
        in_specs=(rows, rows, rows, slabs, slabs, slabs),
        out_specs=rows,
        check_vma=False,
    )
```

```python
import jax
import jax.numpy as jnp
from jax import lax
from jax.sharding import Mesh
from jax.sharding import PartitionSpec as P

SHARERS = 4
RETURN_DTYPE = jnp.bfloat16


def shift(x, axis, size, k):
    return lax.ppermute(x, axis, [(i, (i + k) % size) for i in range(size)])


def quarter_rows(rows, w_gate, w_up, w_down, n_ctx):
    dims = (((1,), (1,)), ((), ()))
    gate = lax.dot_general(rows, w_gate, dims, preferred_element_type=jnp.float32)
    up = lax.dot_general(rows, w_up, dims, preferred_element_type=jnp.float32)
    hidden = (jax.nn.silu(gate) * up).astype(jnp.bfloat16)
    slab = w_down.shape[0] // n_ctx
    total = None
    for c in range(n_ctx):
        part = jnp.dot(
            hidden[:, c * slab : (c + 1) * slab],
            w_down[c * slab : (c + 1) * slab],
            preferred_element_type=jnp.float32,
        ).astype(jnp.bfloat16)
        total = part.astype(jnp.float32) if total is None else total + part.astype(jnp.float32)
    return total


def per_device(tokens, routes, route_weight, w_gate, w_up, w_down):
    tok = tokens.shape[0]
    top = routes.shape[1]
    width = tokens.shape[1]
    experts = lax.axis_size("ex")
    sharers = lax.axis_size("sh")
    n_ctx = lax.axis_size("context")
    route_count = max(5 * experts, 2 * top)
    capacity = max(2, 5 * tok * top // (2 * route_count))
    half = -(-capacity // n_ctx)
    span = n_ctx * half
    ctx = lax.axis_index("context")
    me = lax.axis_index("ex")

    def with_sibling(x):
        return jnp.concatenate([x, shift(x, "context", n_ctx, 1)], axis=0)

    wg = with_sibling(w_gate[0])
    wu = with_sibling(w_up[0])
    wd = with_sibling(w_down[0])

    other_routes = shift(routes, "context", n_ctx, 1)
    pair_routes = jnp.where(
        ctx == 0,
        jnp.concatenate([routes, other_routes], axis=0),
        jnp.concatenate([other_routes, routes], axis=0),
    )
    flat = pair_routes.reshape(-1)
    onehot = (flat[:, None] == jnp.arange(experts, dtype=jnp.int32)[None, :]).astype(jnp.int32)
    earlier = jnp.cumsum(onehot, axis=0) - onehot
    slot = jnp.sum(earlier * onehot, axis=1)
    real = flat < experts
    cell = jnp.where(real, flat * span + slot, experts * span)
    pair_cell = cell.reshape(n_ctx * tok, top)
    local_cell = jnp.where(ctx == 0, pair_cell, jnp.roll(pair_cell, tok, axis=0))

    if experts == 2:
        expert_order = jnp.stack([me, 1 - me])
    else:
        expert_order = jnp.arange(experts, dtype=jnp.int32)
    own_cells = (
        expert_order[:, None] * span + ctx * half + jnp.arange(half, dtype=jnp.int32)[None, :]
    ).reshape(-1)
    match = local_cell[None, :, :] == own_cells[:, None, None]
    picker = jnp.sum(match.astype(jnp.float32), axis=2).astype(jnp.bfloat16)
    pair_tokens = with_sibling(tokens)
    packed = jnp.dot(picker, pair_tokens, preferred_element_type=jnp.float32).astype(jnp.bfloat16)
    packed = packed.reshape(experts, half, width)

    def group_partial(sent):
        group = [sent] + [shift(sent, "sh", sharers, k) for k in range(1, sharers)]
        rows = jnp.stack(group).reshape(-1, width)
        partial = quarter_rows(rows, wg, wu, wd, n_ctx).astype(jnp.bfloat16)
        return partial.reshape((sharers,) + sent.shape)

    def group_sum(partial):
        total = partial[0].astype(jnp.float32)
        for k in range(1, sharers):
            total = total + shift(partial[k], "sh", sharers, -k).astype(jnp.float32)
        return total

    if experts == 2:
        local_part = group_partial(packed[0:1])
        far_part = group_partial(shift(packed[1:2], "ex", 2, 1))
        far_out = group_sum(far_part)
        local_part, far_out = lax.optimization_barrier((local_part, far_out))
        back = shift(far_out.astype(RETURN_DTYPE), "ex", 2, 1).astype(jnp.float32)
        mine = jnp.concatenate([group_sum(local_part), back], axis=0)
    else:
        sent = lax.all_to_all(packed, "ex", split_axis=0, concat_axis=0, tiled=True)
        expert_out = group_sum(group_partial(sent)).astype(RETURN_DTYPE)
        mine = lax.all_to_all(expert_out, "ex", split_axis=0, concat_axis=0, tiled=True)
        mine = mine.astype(jnp.float32)
    theirs = shift(mine, "context", n_ctx, 1)
    slots_out = jnp.concatenate([mine, theirs], axis=0).reshape(n_ctx * experts * half, width)

    own_cell = local_cell[:tok]
    expert_of = own_cell // span
    slot_of = own_cell % span
    if experts == 2:
        position = jnp.where(expert_of == me, 0, 1)
    else:
        position = expert_of
    block = jnp.where(slot_of // half == ctx, 0, 1)
    layout = block * (experts * half) + position * half + slot_of % half
    layout = jnp.where(own_cell < experts * span, layout, n_ctx * experts * half)
    own_match = (
        layout[:, :, None] == jnp.arange(n_ctx * experts * half, dtype=jnp.int32)[None, None, :]
    ).astype(jnp.float32)
    mixing = jnp.sum(own_match * route_weight[:, :, None], axis=1)
    mixed = jnp.dot(
        mixing, slots_out, precision=lax.Precision.HIGHEST, preferred_element_type=jnp.float32
    )
    return mixed.astype(jnp.bfloat16)


def solution(mesh):
    groups, n_expert, n_ctx = mesh.devices.shape
    split = Mesh(
        mesh.devices.reshape(groups, n_expert // SHARERS, SHARERS, n_ctx),
        ("groups", "ex", "sh", "context"),
    )
    rows = P(("groups", "ex", "sh", "context"), None)
    slabs = P(("ex", "sh"), "context", None)
    return jax.shard_map(
        per_device,
        mesh=split,
        in_specs=(rows, rows, rows, slabs, slabs, slabs),
        out_specs=rows,
        check_vma=False,
    )
```

```python
import jax
import jax.numpy as jnp
from jax import lax
from jax.sharding import Mesh
from jax.sharding import PartitionSpec as P

SHARERS = 4
RETURN_DTYPE = jnp.bfloat16


def shift(x, axis, size, k):
    return lax.ppermute(x, axis, [(i, (i + k) % size) for i in range(size)])


def quarter_rows(rows, w_gate, w_up, w_down, n_ctx):
    dims = (((1,), (1,)), ((), ()))
    gate = lax.dot_general(rows, w_gate, dims, preferred_element_type=jnp.float32)
    up = lax.dot_general(rows, w_up, dims, preferred_element_type=jnp.float32)
    hidden = (jax.nn.silu(gate) * up).astype(jnp.bfloat16)
    slab = w_down.shape[0] // n_ctx
    total = None
    for c in range(n_ctx):
        part = jnp.dot(
            hidden[:, c * slab : (c + 1) * slab],
            w_down[c * slab : (c + 1) * slab],
            preferred_element_type=jnp.float32,
        ).astype(jnp.bfloat16)
        total = part.astype(jnp.float32) if total is None else total + part.astype(jnp.float32)
    return total


def per_device(tokens, routes, route_weight, w_gate, w_up, w_down):
    tok = tokens.shape[0]
    top = routes.shape[1]
    width = tokens.shape[1]
    experts = lax.axis_size("ex")
    sharers = lax.axis_size("sh")
    n_ctx = lax.axis_size("context")
    route_count = max(5 * experts, 2 * top)
    capacity = max(2, 5 * tok * top // (2 * route_count))
    half = -(-capacity // n_ctx)
    span = n_ctx * half
    ctx = lax.axis_index("context")
    me = lax.axis_index("ex")

    def with_sibling(x):
        return jnp.concatenate([x, shift(x, "context", n_ctx, 1)], axis=0)

    slabs = jnp.stack([w_gate[0], w_up[0], w_down[0]])
    quarter = jnp.concatenate([slabs, shift(slabs, "context", n_ctx, 1)], axis=1)
    wg, wu, wd = quarter[0], quarter[1], quarter[2]

    other_routes = shift(routes, "context", n_ctx, 1)
    pair_routes = jnp.where(
        ctx == 0,
        jnp.concatenate([routes, other_routes], axis=0),
        jnp.concatenate([other_routes, routes], axis=0),
    )
    flat = pair_routes.reshape(-1)
    onehot = (flat[:, None] == jnp.arange(experts, dtype=jnp.int32)[None, :]).astype(jnp.int32)
    earlier = jnp.cumsum(onehot, axis=0) - onehot
    slot = jnp.sum(earlier * onehot, axis=1)
    real = flat < experts
    cell = jnp.where(real, flat * span + slot, experts * span)
    pair_cell = cell.reshape(n_ctx * tok, top)
    local_cell = jnp.where(ctx == 0, pair_cell, jnp.roll(pair_cell, tok, axis=0))

    if experts == 2:
        expert_order = jnp.stack([me, 1 - me])
    else:
        expert_order = jnp.arange(experts, dtype=jnp.int32)
    own_cells = (
        expert_order[:, None] * span + ctx * half + jnp.arange(half, dtype=jnp.int32)[None, :]
    ).reshape(-1)
    match = local_cell[None, :, :] == own_cells[:, None, None]
    picker = jnp.sum(match.astype(jnp.float32), axis=2).astype(jnp.bfloat16)
    pair_tokens = with_sibling(tokens)
    packed = jnp.dot(picker, pair_tokens, preferred_element_type=jnp.float32).astype(jnp.bfloat16)
    packed = packed.reshape(experts, half, width)

    def group_partial(sent):
        group = [sent] + [shift(sent, "sh", sharers, k) for k in range(1, sharers)]
        rows = jnp.stack(group).reshape(-1, width)
        partial = quarter_rows(rows, wg, wu, wd, n_ctx).astype(jnp.bfloat16)
        return partial.reshape((sharers,) + sent.shape)

    def group_sum(partial):
        total = partial[0].astype(jnp.float32)
        for k in range(1, sharers):
            total = total + shift(partial[k], "sh", sharers, -k).astype(jnp.float32)
        return total

    if experts == 2:
        far_sent = shift(packed[1:2], "ex", 2, 1)
        local_part = group_partial(packed[0:1])
        local_part, far_sent = lax.optimization_barrier((local_part, far_sent))
        far_part = group_partial(far_sent)
        far_out = group_sum(far_part)
        local_part, far_out = lax.optimization_barrier((local_part, far_out))
        back = shift(far_out.astype(RETURN_DTYPE), "ex", 2, 1).astype(jnp.float32)
        mine = jnp.concatenate([group_sum(local_part), back], axis=0)
    else:
        sent = lax.all_to_all(packed, "ex", split_axis=0, concat_axis=0, tiled=True)
        expert_out = group_sum(group_partial(sent)).astype(RETURN_DTYPE)
        mine = lax.all_to_all(expert_out, "ex", split_axis=0, concat_axis=0, tiled=True)
        mine = mine.astype(jnp.float32)
    theirs = shift(mine, "context", n_ctx, 1)
    slots_out = jnp.concatenate([mine, theirs], axis=0).reshape(n_ctx * experts * half, width)

    own_cell = local_cell[:tok]
    expert_of = own_cell // span
    slot_of = own_cell % span
    if experts == 2:
        position = jnp.where(expert_of == me, 0, 1)
    else:
        position = expert_of
    block = jnp.where(slot_of // half == ctx, 0, 1)
    layout = block * (experts * half) + position * half + slot_of % half
    layout = jnp.where(own_cell < experts * span, layout, n_ctx * experts * half)
    own_match = (
        layout[:, :, None] == jnp.arange(n_ctx * experts * half, dtype=jnp.int32)[None, None, :]
    ).astype(jnp.float32)
    mixing = jnp.sum(own_match * route_weight[:, :, None], axis=1)
    mixed = jnp.dot(
        mixing, slots_out, precision=lax.Precision.HIGHEST, preferred_element_type=jnp.float32
    )
    return mixed.astype(jnp.bfloat16)


def solution(mesh):
    groups, n_expert, n_ctx = mesh.devices.shape
    split = Mesh(
        mesh.devices.reshape(groups, n_expert // SHARERS, SHARERS, n_ctx),
        ("groups", "ex", "sh", "context"),
    )
    rows = P(("groups", "ex", "sh", "context"), None)
    slabs = P(("ex", "sh"), "context", None)
    return jax.shard_map(
        per_device,
        mesh=split,
        in_specs=(rows, rows, rows, slabs, slabs, slabs),
        out_specs=rows,
        check_vma=False,
    )
```

```python
import jax
import jax.numpy as jnp
from jax import lax
from jax.sharding import Mesh
from jax.sharding import PartitionSpec as P

SHARERS = 4
RETURN_DTYPE = jnp.bfloat16


def shift(x, axis, size, k):
    return lax.ppermute(x, axis, [(i, (i + k) % size) for i in range(size)])


def swap(x, axis, size, k):
    return lax.ppermute(x, axis, [(i, i ^ k) for i in range(size)])


def quarter_rows(rows, w_gate, w_up, w_down, n_ctx):
    dims = (((1,), (1,)), ((), ()))
    gate = lax.dot_general(rows, w_gate, dims, preferred_element_type=jnp.float32)
    up = lax.dot_general(rows, w_up, dims, preferred_element_type=jnp.float32)
    hidden = (jax.nn.silu(gate) * up).astype(jnp.bfloat16)
    slab = w_down.shape[0] // n_ctx
    total = None
    for c in range(n_ctx):
        part = jnp.dot(
            hidden[:, c * slab : (c + 1) * slab],
            w_down[c * slab : (c + 1) * slab],
            preferred_element_type=jnp.float32,
        ).astype(jnp.bfloat16)
        total = part.astype(jnp.float32) if total is None else total + part.astype(jnp.float32)
    return total


def per_device(tokens, routes, route_weight, w_gate, w_up, w_down):
    tok = tokens.shape[0]
    top = routes.shape[1]
    width = tokens.shape[1]
    experts = lax.axis_size("ex")
    sharers = lax.axis_size("sh")
    n_ctx = lax.axis_size("context")
    route_count = max(5 * experts, 2 * top)
    capacity = max(2, 5 * tok * top // (2 * route_count))
    half = -(-capacity // n_ctx)
    span = n_ctx * half
    ctx = lax.axis_index("context")
    me = lax.axis_index("ex")

    def with_sibling(x):
        return jnp.concatenate([x, shift(x, "context", n_ctx, 1)], axis=0)

    wg = with_sibling(w_gate[0])
    wu = with_sibling(w_up[0])
    wd = with_sibling(w_down[0])

    other_routes = shift(routes, "context", n_ctx, 1)
    pair_routes = jnp.where(
        ctx == 0,
        jnp.concatenate([routes, other_routes], axis=0),
        jnp.concatenate([other_routes, routes], axis=0),
    )
    flat = pair_routes.reshape(-1)
    onehot = (flat[:, None] == jnp.arange(experts, dtype=jnp.int32)[None, :]).astype(jnp.int32)
    earlier = jnp.cumsum(onehot, axis=0) - onehot
    slot = jnp.sum(earlier * onehot, axis=1)
    real = flat < experts
    cell = jnp.where(real, flat * span + slot, experts * span)
    pair_cell = cell.reshape(n_ctx * tok, top)
    local_cell = jnp.where(ctx == 0, pair_cell, jnp.roll(pair_cell, tok, axis=0))

    if experts == 2:
        expert_order = jnp.stack([me, 1 - me])
    else:
        expert_order = jnp.arange(experts, dtype=jnp.int32)
    own_cells = (
        expert_order[:, None] * span + ctx * half + jnp.arange(half, dtype=jnp.int32)[None, :]
    ).reshape(-1)
    match = local_cell[None, :, :] == own_cells[:, None, None]
    picker = jnp.sum(match.astype(jnp.float32), axis=2).astype(jnp.bfloat16)
    pair_tokens = with_sibling(tokens)
    packed = jnp.dot(picker, pair_tokens, preferred_element_type=jnp.float32).astype(jnp.bfloat16)
    packed = packed.reshape(experts, half, width)

    def exchange(x, k):
        if sharers & (sharers - 1) == 0:
            return swap(x, "sh", sharers, k)
        return shift(x, "sh", sharers, k)

    def back_exchange(x, k):
        if sharers & (sharers - 1) == 0:
            return swap(x, "sh", sharers, k)
        return shift(x, "sh", sharers, -k)

    def group_partial(sent):
        group = [sent] + [exchange(sent, k) for k in range(1, sharers)]
        rows = jnp.stack(group).reshape(-1, width)
        partial = quarter_rows(rows, wg, wu, wd, n_ctx).astype(jnp.bfloat16)
        return partial.reshape((sharers,) + sent.shape)

    def group_sum(partial):
        total = partial[0].astype(jnp.float32)
        for k in range(1, sharers):
            total = total + back_exchange(partial[k], k).astype(jnp.float32)
        return total

    if experts == 2:
        local_part = group_partial(packed[0:1])
        far_part = group_partial(shift(packed[1:2], "ex", 2, 1))
        far_out = group_sum(far_part)
        local_part, far_out = lax.optimization_barrier((local_part, far_out))
        back = shift(far_out.astype(RETURN_DTYPE), "ex", 2, 1).astype(jnp.float32)
        mine = jnp.concatenate([group_sum(local_part), back], axis=0)
    else:
        sent = lax.all_to_all(packed, "ex", split_axis=0, concat_axis=0, tiled=True)
        expert_out = group_sum(group_partial(sent)).astype(RETURN_DTYPE)
        mine = lax.all_to_all(expert_out, "ex", split_axis=0, concat_axis=0, tiled=True)
        mine = mine.astype(jnp.float32)
    theirs = shift(mine, "context", n_ctx, 1)
    slots_out = jnp.concatenate([mine, theirs], axis=0).reshape(n_ctx * experts * half, width)

    own_cell = local_cell[:tok]
    expert_of = own_cell // span
    slot_of = own_cell % span
    if experts == 2:
        position = jnp.where(expert_of == me, 0, 1)
    else:
        position = expert_of
    block = jnp.where(slot_of // half == ctx, 0, 1)
    layout = block * (experts * half) + position * half + slot_of % half
    layout = jnp.where(own_cell < experts * span, layout, n_ctx * experts * half)
    own_match = (
        layout[:, :, None] == jnp.arange(n_ctx * experts * half, dtype=jnp.int32)[None, None, :]
    ).astype(jnp.float32)
    mixing = jnp.sum(own_match * route_weight[:, :, None], axis=1)
    mixed = jnp.dot(
        mixing, slots_out, precision=lax.Precision.HIGHEST, preferred_element_type=jnp.float32
    )
    return mixed.astype(jnp.bfloat16)


def solution(mesh):
    groups, n_expert, n_ctx = mesh.devices.shape
    split = Mesh(
        mesh.devices.reshape(groups, n_expert // SHARERS, SHARERS, n_ctx),
        ("groups", "ex", "sh", "context"),
    )
    rows = P(("groups", "ex", "sh", "context"), None)
    slabs = P(("ex", "sh"), "context", None)
    return jax.shard_map(
        per_device,
        mesh=split,
        in_specs=(rows, rows, rows, slabs, slabs, slabs),
        out_specs=rows,
        check_vma=False,
    )
```

```python
import jax
import jax.numpy as jnp
from jax import lax
from jax.sharding import Mesh
from jax.sharding import PartitionSpec as P

SHARERS = 4
RETURN_DTYPE = jnp.bfloat16


def shift(x, axis, size, k):
    return lax.ppermute(x, axis, [(i, (i + k) % size) for i in range(size)])


def swap(x, axis, size, k):
    return lax.ppermute(x, axis, [(i, i ^ k) for i in range(size)])


def quarter_rows(rows, w_gate, w_up, w_down, n_ctx):
    dims = (((1,), (1,)), ((), ()))
    gate = lax.dot_general(rows, w_gate, dims, preferred_element_type=jnp.float32)
    up = lax.dot_general(rows, w_up, dims, preferred_element_type=jnp.float32)
    hidden = (jax.nn.silu(gate) * up).astype(jnp.bfloat16)
    slab = w_down.shape[0] // n_ctx
    total = None
    for c in range(n_ctx):
        part = jnp.dot(
            hidden[:, c * slab : (c + 1) * slab],
            w_down[c * slab : (c + 1) * slab],
            preferred_element_type=jnp.float32,
        ).astype(jnp.bfloat16)
        total = part.astype(jnp.float32) if total is None else total + part.astype(jnp.float32)
    return total


def per_device(tokens, routes, route_weight, w_gate, w_up, w_down):
    tok = tokens.shape[0]
    top = routes.shape[1]
    width = tokens.shape[1]
    experts = lax.axis_size("ex")
    sharers = lax.axis_size("sh")
    n_ctx = lax.axis_size("context")
    route_count = max(5 * experts, 2 * top)
    capacity = max(2, 5 * tok * top // (2 * route_count))
    half = -(-capacity // n_ctx)
    span = n_ctx * half
    ctx = lax.axis_index("context")
    me = lax.axis_index("ex")

    def with_sibling(x):
        return jnp.concatenate([x, shift(x, "context", n_ctx, 1)], axis=0)

    wg = with_sibling(w_gate[0])
    wu = with_sibling(w_up[0])
    wd = with_sibling(w_down[0])

    other_routes = shift(routes, "context", n_ctx, 1)
    pair_routes = jnp.where(
        ctx == 0,
        jnp.concatenate([routes, other_routes], axis=0),
        jnp.concatenate([other_routes, routes], axis=0),
    )
    flat = pair_routes.reshape(-1)
    onehot = (flat[:, None] == jnp.arange(experts, dtype=jnp.int32)[None, :]).astype(jnp.int32)
    earlier = jnp.cumsum(onehot, axis=0) - onehot
    slot = jnp.sum(earlier * onehot, axis=1)
    real = flat < experts
    cell = jnp.where(real, flat * span + slot, experts * span)
    pair_cell = cell.reshape(n_ctx * tok, top)
    local_cell = jnp.where(ctx == 0, pair_cell, jnp.roll(pair_cell, tok, axis=0))

    if experts == 2:
        expert_order = jnp.stack([me, 1 - me])
    else:
        expert_order = jnp.arange(experts, dtype=jnp.int32)
    own_cells = (
        expert_order[:, None] * span + ctx * half + jnp.arange(half, dtype=jnp.int32)[None, :]
    ).reshape(-1)
    match = local_cell[None, :, :] == own_cells[:, None, None]
    picker = jnp.sum(match.astype(jnp.float32), axis=2).astype(jnp.bfloat16)
    pair_tokens = with_sibling(tokens)
    packed = jnp.dot(picker, pair_tokens, preferred_element_type=jnp.float32).astype(jnp.bfloat16)
    packed = packed.reshape(experts, half, width)

    def exchange(x, k):
        if sharers & (sharers - 1) == 0:
            return swap(x, "sh", sharers, k)
        return shift(x, "sh", sharers, k)

    def back_exchange(x, k):
        if sharers & (sharers - 1) == 0:
            return swap(x, "sh", sharers, k)
        return shift(x, "sh", sharers, -k)

    def group_partial(sent):
        group = [sent] + [exchange(sent, k) for k in range(1, sharers)]
        rows = jnp.stack(group).reshape(-1, width)
        partial = quarter_rows(rows, wg, wu, wd, n_ctx).astype(jnp.bfloat16)
        return partial.reshape((sharers,) + sent.shape)

    def group_sum(partial):
        total = partial[0].astype(jnp.float32)
        for k in range(1, sharers):
            total = total + back_exchange(partial[k], k).astype(jnp.float32)
        return total

    if experts == 2:
        cut = half // 2 + (half // 2) % 8 if half >= 16 else half
        pieces = [(0, cut)] + ([(cut, half)] if cut < half else [])
        local_part = group_partial(packed[0:1])
        far_out = [
            group_sum(group_partial(shift(packed[1:2, lo:hi], "ex", 2, 1))) for lo, hi in pieces
        ]
        local_part, far_out = lax.optimization_barrier((local_part, far_out))
        back = [shift(o.astype(RETURN_DTYPE), "ex", 2, 1).astype(jnp.float32) for o in far_out]
        mine = jnp.concatenate([group_sum(local_part), jnp.concatenate(back, axis=1)], axis=0)
    else:
        sent = lax.all_to_all(packed, "ex", split_axis=0, concat_axis=0, tiled=True)
        expert_out = group_sum(group_partial(sent)).astype(RETURN_DTYPE)
        mine = lax.all_to_all(expert_out, "ex", split_axis=0, concat_axis=0, tiled=True)
        mine = mine.astype(jnp.float32)
    theirs = shift(mine, "context", n_ctx, 1)
    slots_out = jnp.concatenate([mine, theirs], axis=0).reshape(n_ctx * experts * half, width)

    own_cell = local_cell[:tok]
    expert_of = own_cell // span
    slot_of = own_cell % span
    if experts == 2:
        position = jnp.where(expert_of == me, 0, 1)
    else:
        position = expert_of
    block = jnp.where(slot_of // half == ctx, 0, 1)
    layout = block * (experts * half) + position * half + slot_of % half
    layout = jnp.where(own_cell < experts * span, layout, n_ctx * experts * half)
    own_match = (
        layout[:, :, None] == jnp.arange(n_ctx * experts * half, dtype=jnp.int32)[None, None, :]
    ).astype(jnp.float32)
    mixing = jnp.sum(own_match * route_weight[:, :, None], axis=1)
    mixed = jnp.dot(
        mixing, slots_out, precision=lax.Precision.HIGHEST, preferred_element_type=jnp.float32
    )
    return mixed.astype(jnp.bfloat16)


def solution(mesh):
    groups, n_expert, n_ctx = mesh.devices.shape
    split = Mesh(
        mesh.devices.reshape(groups, n_expert // SHARERS, SHARERS, n_ctx),
        ("groups", "ex", "sh", "context"),
    )
    rows = P(("groups", "ex", "sh", "context"), None)
    slabs = P(("ex", "sh"), "context", None)
    return jax.shard_map(
        per_device,
        mesh=split,
        in_specs=(rows, rows, rows, slabs, slabs, slabs),
        out_specs=rows,
        check_vma=False,
    )
```

```python
import jax
import jax.numpy as jnp
from jax import lax
from jax.sharding import Mesh
from jax.sharding import PartitionSpec as P

SHARERS = 4
RETURN_DTYPE = jnp.bfloat16


def shift(x, axis, size, k):
    return lax.ppermute(x, axis, [(i, (i + k) % size) for i in range(size)])


def swap(x, axis, size, k):
    return lax.ppermute(x, axis, [(i, i ^ k) for i in range(size)])


def slab_rows(rows, w_gate, w_up, w_down):
    dims = (((1,), (1,)), ((), ()))
    gate = lax.dot_general(rows, w_gate, dims, preferred_element_type=jnp.float32)
    up = lax.dot_general(rows, w_up, dims, preferred_element_type=jnp.float32)
    hidden = (jax.nn.silu(gate) * up).astype(jnp.bfloat16)
    part = jnp.dot(hidden, w_down, preferred_element_type=jnp.float32).astype(jnp.bfloat16)
    return part.astype(jnp.float32)


def per_device(tokens, routes, route_weight, w_gate, w_up, w_down):
    tok = tokens.shape[0]
    top = routes.shape[1]
    width = tokens.shape[1]
    experts = lax.axis_size("ex")
    sharers = lax.axis_size("sh")
    n_ctx = lax.axis_size("context")
    route_count = max(5 * experts, 2 * top)
    capacity = max(2, 5 * tok * top // (2 * route_count))
    half = -(-capacity // n_ctx)
    span = n_ctx * half
    ctx = lax.axis_index("context")
    me = lax.axis_index("ex")

    own_slab = (w_gate[0], w_up[0], w_down[0])
    other_slab = tuple(shift(w, "context", n_ctx, 1) for w in own_slab)

    def with_sibling(x):
        return jnp.concatenate([x, shift(x, "context", n_ctx, 1)], axis=0)

    other_routes = shift(routes, "context", n_ctx, 1)
    pair_routes = jnp.where(
        ctx == 0,
        jnp.concatenate([routes, other_routes], axis=0),
        jnp.concatenate([other_routes, routes], axis=0),
    )
    flat = pair_routes.reshape(-1)
    onehot = (flat[:, None] == jnp.arange(experts, dtype=jnp.int32)[None, :]).astype(jnp.int32)
    earlier = jnp.cumsum(onehot, axis=0) - onehot
    slot = jnp.sum(earlier * onehot, axis=1)
    real = flat < experts
    cell = jnp.where(real, flat * span + slot, experts * span)
    pair_cell = cell.reshape(n_ctx * tok, top)
    local_cell = jnp.where(ctx == 0, pair_cell, jnp.roll(pair_cell, tok, axis=0))

    if experts == 2:
        expert_order = jnp.stack([me, 1 - me])
    else:
        expert_order = jnp.arange(experts, dtype=jnp.int32)
    own_cells = (
        expert_order[:, None] * span + ctx * half + jnp.arange(half, dtype=jnp.int32)[None, :]
    ).reshape(-1)
    match = local_cell[None, :, :] == own_cells[:, None, None]
    picker = jnp.sum(match.astype(jnp.float32), axis=2).astype(jnp.bfloat16)
    pair_tokens = with_sibling(tokens)
    packed = jnp.dot(picker, pair_tokens, preferred_element_type=jnp.float32).astype(jnp.bfloat16)
    packed = packed.reshape(experts, half, width)

    def exchange(x, k):
        if sharers & (sharers - 1) == 0:
            return swap(x, "sh", sharers, k)
        return shift(x, "sh", sharers, k)

    def back_exchange(x, k):
        if sharers & (sharers - 1) == 0:
            return swap(x, "sh", sharers, k)
        return shift(x, "sh", sharers, -k)

    def group_partial(sent):
        group = [sent] + [exchange(sent, k) for k in range(1, sharers)]
        rows = jnp.stack(group).reshape(-1, width)
        partial = (slab_rows(rows, *own_slab) + slab_rows(rows, *other_slab)).astype(jnp.bfloat16)
        return partial.reshape((sharers,) + sent.shape)

    def group_sum(partial):
        total = partial[0].astype(jnp.float32)
        for k in range(1, sharers):
            total = total + back_exchange(partial[k], k).astype(jnp.float32)
        return total

    if experts == 2:
        local_part = group_partial(packed[0:1])
        far_part = group_partial(shift(packed[1:2], "ex", 2, 1))
        far_out = group_sum(far_part)
        local_part, far_out = lax.optimization_barrier((local_part, far_out))
        back = shift(far_out.astype(RETURN_DTYPE), "ex", 2, 1).astype(jnp.float32)
        mine = jnp.concatenate([group_sum(local_part), back], axis=0)
    else:
        sent = lax.all_to_all(packed, "ex", split_axis=0, concat_axis=0, tiled=True)
        expert_out = group_sum(group_partial(sent)).astype(RETURN_DTYPE)
        mine = lax.all_to_all(expert_out, "ex", split_axis=0, concat_axis=0, tiled=True)
        mine = mine.astype(jnp.float32)
    theirs = shift(mine, "context", n_ctx, 1)
    slots_out = jnp.concatenate([mine, theirs], axis=0).reshape(n_ctx * experts * half, width)

    own_cell = local_cell[:tok]
    expert_of = own_cell // span
    slot_of = own_cell % span
    if experts == 2:
        position = jnp.where(expert_of == me, 0, 1)
    else:
        position = expert_of
    block = jnp.where(slot_of // half == ctx, 0, 1)
    layout = block * (experts * half) + position * half + slot_of % half
    layout = jnp.where(own_cell < experts * span, layout, n_ctx * experts * half)
    own_match = (
        layout[:, :, None] == jnp.arange(n_ctx * experts * half, dtype=jnp.int32)[None, None, :]
    ).astype(jnp.float32)
    mixing = jnp.sum(own_match * route_weight[:, :, None], axis=1)
    mixed = jnp.dot(
        mixing, slots_out, precision=lax.Precision.HIGHEST, preferred_element_type=jnp.float32
    )
    return mixed.astype(jnp.bfloat16)


def solution(mesh):
    groups, n_expert, n_ctx = mesh.devices.shape
    split = Mesh(
        mesh.devices.reshape(groups, n_expert // SHARERS, SHARERS, n_ctx),
        ("groups", "ex", "sh", "context"),
    )
    rows = P(("groups", "ex", "sh", "context"), None)
    slabs = P(("ex", "sh"), "context", None)
    return jax.shard_map(
        per_device,
        mesh=split,
        in_specs=(rows, rows, rows, slabs, slabs, slabs),
        out_specs=rows,
        check_vma=False,
    )
```

```python
import jax
import jax.numpy as jnp
from jax import lax
from jax.sharding import Mesh
from jax.sharding import PartitionSpec as P

SHARERS = 4
RETURN_DTYPE = jnp.bfloat16


def shift(x, axis, size, k):
    return lax.ppermute(x, axis, [(i, (i + k) % size) for i in range(size)])


def swap(x, axis, size, k):
    return lax.ppermute(x, axis, [(i, i ^ k) for i in range(size)])


def quarter_rows(rows, w_gate, w_up, w_down, n_ctx):
    dims = (((1,), (1,)), ((), ()))
    gate = lax.dot_general(rows, w_gate, dims, preferred_element_type=jnp.float32)
    up = lax.dot_general(rows, w_up, dims, preferred_element_type=jnp.float32)
    hidden = (jax.nn.silu(gate) * up).astype(jnp.bfloat16)
    slab = w_down.shape[0] // n_ctx
    total = None
    for c in range(n_ctx):
        part = jnp.dot(
            hidden[:, c * slab : (c + 1) * slab],
            w_down[c * slab : (c + 1) * slab],
            preferred_element_type=jnp.float32,
        ).astype(jnp.bfloat16)
        total = part.astype(jnp.float32) if total is None else total + part.astype(jnp.float32)
    return total


def per_device(tokens, routes, route_weight, w_gate, w_up, w_down):
    tok = tokens.shape[0]
    top = routes.shape[1]
    width = tokens.shape[1]
    experts = lax.axis_size("ex")
    sharers = lax.axis_size("sh")
    n_ctx = lax.axis_size("context")
    route_count = max(5 * experts, 2 * top)
    capacity = max(2, 5 * tok * top // (2 * route_count))
    half = -(-capacity // n_ctx)
    span = n_ctx * half
    ctx = lax.axis_index("context")
    me = lax.axis_index("ex")

    def with_sibling(x):
        return jnp.concatenate([x, shift(x, "context", n_ctx, 1)], axis=0)

    wg = with_sibling(w_gate[0])
    wu = with_sibling(w_up[0])
    wd = with_sibling(w_down[0])

    other_routes = shift(routes, "context", n_ctx, 1)
    pair_routes = jnp.where(
        ctx == 0,
        jnp.concatenate([routes, other_routes], axis=0),
        jnp.concatenate([other_routes, routes], axis=0),
    )
    flat = pair_routes.reshape(-1)
    onehot = (flat[:, None] == jnp.arange(experts, dtype=jnp.int32)[None, :]).astype(jnp.int32)
    earlier = jnp.cumsum(onehot, axis=0) - onehot
    slot = jnp.sum(earlier * onehot, axis=1)
    real = flat < experts
    cell = jnp.where(real, flat * span + slot, experts * span)
    pair_cell = cell.reshape(n_ctx * tok, top)
    local_cell = jnp.where(ctx == 0, pair_cell, jnp.roll(pair_cell, tok, axis=0))

    if experts == 2:
        expert_order = jnp.stack([me, 1 - me])
    else:
        expert_order = jnp.arange(experts, dtype=jnp.int32)
    own_cells = (
        expert_order[:, None] * span + ctx * half + jnp.arange(half, dtype=jnp.int32)[None, :]
    ).reshape(-1)
    match = local_cell[None, :, :] == own_cells[:, None, None]
    picker = jnp.sum(match.astype(jnp.float32), axis=2).astype(jnp.bfloat16)
    pair_tokens = with_sibling(tokens)
    packed = jnp.dot(picker, pair_tokens, preferred_element_type=jnp.float32).astype(jnp.bfloat16)
    packed = packed.reshape(experts, half, width)

    def exchange(x, k):
        if sharers & (sharers - 1) == 0:
            return swap(x, "sh", sharers, k)
        return shift(x, "sh", sharers, k)

    def back_exchange(x, k):
        if sharers & (sharers - 1) == 0:
            return swap(x, "sh", sharers, k)
        return shift(x, "sh", sharers, -k)

    def group_partial(sent):
        group = [sent] + [exchange(sent, k) for k in range(1, sharers)]
        rows = jnp.stack(group).reshape(-1, width)
        partial = quarter_rows(rows, wg, wu, wd, n_ctx).astype(jnp.bfloat16)
        return partial.reshape((sharers,) + sent.shape)

    def group_sum(partial):
        total = partial[0].astype(jnp.float32)
        for k in range(1, sharers):
            total = total + back_exchange(partial[k], k).astype(jnp.float32)
        return total

    if experts == 2:
        local_part = group_partial(packed[0:1])
        far_part = group_partial(shift(packed[1:2], "ex", 2, 1))
        far_out = group_sum(far_part)
        local_part, far_out = lax.optimization_barrier((local_part, far_out))
        back = shift(far_out.astype(RETURN_DTYPE), "ex", 2, 1).astype(jnp.float32)
        mine = jnp.concatenate([group_sum(local_part), back], axis=0)
    else:
        sent = lax.all_to_all(packed, "ex", split_axis=0, concat_axis=0, tiled=True)
        expert_out = group_sum(group_partial(sent)).astype(RETURN_DTYPE)
        mine = lax.all_to_all(expert_out, "ex", split_axis=0, concat_axis=0, tiled=True)
        mine = mine.astype(jnp.float32)
    theirs = shift(mine, "context", n_ctx, 1)
    slots_out = jnp.concatenate([mine, theirs], axis=0).reshape(n_ctx * experts * half, width)

    own_cell = local_cell[:tok]
    expert_of = own_cell // span
    slot_of = own_cell % span
    if experts == 2:
        position = jnp.where(expert_of == me, 0, 1)
    else:
        position = expert_of
    block = jnp.where(slot_of // half == ctx, 0, 1)
    layout = block * (experts * half) + position * half + slot_of % half
    layout = jnp.where(own_cell < experts * span, layout, n_ctx * experts * half)
    own_match = (
        layout[:, :, None] == jnp.arange(n_ctx * experts * half, dtype=jnp.int32)[None, None, :]
    ).astype(jnp.float32)
    mixing = jnp.sum(own_match * route_weight[:, :, None], axis=1)
    mixed = jnp.dot(
        mixing, slots_out, precision=lax.Precision.HIGH, preferred_element_type=jnp.float32
    )
    return mixed.astype(jnp.bfloat16)


def solution(mesh):
    groups, n_expert, n_ctx = mesh.devices.shape
    split = Mesh(
        mesh.devices.reshape(groups, n_expert // SHARERS, SHARERS, n_ctx),
        ("groups", "ex", "sh", "context"),
    )
    rows = P(("groups", "ex", "sh", "context"), None)
    slabs = P(("ex", "sh"), "context", None)
    return jax.shard_map(
        per_device,
        mesh=split,
        in_specs=(rows, rows, rows, slabs, slabs, slabs),
        out_specs=rows,
        check_vma=False,
    )
```

```python
import jax
import jax.numpy as jnp
from jax import lax
from jax.sharding import Mesh
from jax.sharding import PartitionSpec as P

SHARERS = 4
RETURN_DTYPE = jnp.bfloat16


def shift(x, axis, size, k):
    return lax.ppermute(x, axis, [(i, (i + k) % size) for i in range(size)])


def swap(x, axis, size, k):
    return lax.ppermute(x, axis, [(i, i ^ k) for i in range(size)])


def quarter_rows(rows, w_gate, w_up, w_down, n_ctx):
    dims = (((1,), (1,)), ((), ()))
    gate = lax.dot_general(rows, w_gate, dims, preferred_element_type=jnp.float32)
    up = lax.dot_general(rows, w_up, dims, preferred_element_type=jnp.float32)
    hidden = (jax.nn.silu(gate) * up).astype(jnp.bfloat16)
    slab = w_down.shape[0] // n_ctx
    total = None
    for c in range(n_ctx):
        part = jnp.dot(
            hidden[:, c * slab : (c + 1) * slab],
            w_down[c * slab : (c + 1) * slab],
            preferred_element_type=jnp.float32,
        ).astype(jnp.bfloat16)
        total = part.astype(jnp.float32) if total is None else total + part.astype(jnp.float32)
    return total


def per_device(tokens, routes, route_weight, w_gate, w_up, w_down):
    tok = tokens.shape[0]
    top = routes.shape[1]
    width = tokens.shape[1]
    experts = lax.axis_size("ex")
    sharers = lax.axis_size("sh")
    n_ctx = lax.axis_size("context")
    route_count = max(5 * experts, 2 * top)
    capacity = max(2, 5 * tok * top // (2 * route_count))
    half = -(-capacity // n_ctx)
    span = n_ctx * half
    ctx = lax.axis_index("context")
    me = lax.axis_index("ex")

    def with_sibling(x):
        return jnp.concatenate([x, shift(x, "context", n_ctx, 1)], axis=0)

    wg = with_sibling(w_gate[0])
    wu = with_sibling(w_up[0])
    wd = with_sibling(w_down[0])

    other_routes = shift(routes, "context", n_ctx, 1)
    pair_routes = jnp.where(
        ctx == 0,
        jnp.concatenate([routes, other_routes], axis=0),
        jnp.concatenate([other_routes, routes], axis=0),
    )
    flat = pair_routes.reshape(-1)
    onehot = (flat[:, None] == jnp.arange(experts, dtype=jnp.int32)[None, :]).astype(jnp.int32)
    earlier = jnp.cumsum(onehot, axis=0) - onehot
    slot = jnp.sum(earlier * onehot, axis=1)
    real = flat < experts
    cell = jnp.where(real, flat * span + slot, experts * span)
    pair_cell = cell.reshape(n_ctx * tok, top)
    local_cell = jnp.where(ctx == 0, pair_cell, jnp.roll(pair_cell, tok, axis=0))

    if experts == 2:
        expert_order = jnp.stack([me, 1 - me])
    else:
        expert_order = jnp.arange(experts, dtype=jnp.int32)
    own_cells = (
        expert_order[:, None] * span + ctx * half + jnp.arange(half, dtype=jnp.int32)[None, :]
    ).reshape(-1)
    match = local_cell[None, :, :] == own_cells[:, None, None]
    picker = jnp.sum(match.astype(jnp.float32), axis=2).astype(jnp.bfloat16)
    pair_tokens = with_sibling(tokens)
    packed = jnp.dot(picker, pair_tokens, preferred_element_type=jnp.float32).astype(jnp.bfloat16)
    packed = packed.reshape(experts, half, width)

    def exchange(x, k):
        if sharers & (sharers - 1) == 0:
            return swap(x, "sh", sharers, k)
        return shift(x, "sh", sharers, k)

    def back_exchange(x, k):
        if sharers & (sharers - 1) == 0:
            return swap(x, "sh", sharers, k)
        return shift(x, "sh", sharers, -k)

    def group_rows(sent):
        return [sent] + [exchange(sent, k) for k in range(1, sharers)]

    def group_partial(group):
        shape = (sharers,) + group[0].shape
        rows = jnp.stack(group).reshape(-1, width)
        partial = quarter_rows(rows, wg, wu, wd, n_ctx).astype(jnp.bfloat16)
        return partial.reshape(shape)

    def group_sum(partial):
        total = partial[0].astype(jnp.float32)
        for k in range(1, sharers):
            total = total + back_exchange(partial[k], k).astype(jnp.float32)
        return total

    if experts == 2:
        local_rows = group_rows(packed[0:1])
        far_rows = group_rows(shift(packed[1:2], "ex", 2, 1))
        both = group_partial([jnp.concatenate(p, axis=0) for p in zip(local_rows, far_rows)])
        local_part, far_part = both[:, 0:1], both[:, 1:2]
        far_out = group_sum(far_part)
        local_part, far_out = lax.optimization_barrier((local_part, far_out))
        back = shift(far_out.astype(RETURN_DTYPE), "ex", 2, 1).astype(jnp.float32)
        mine = jnp.concatenate([group_sum(local_part), back], axis=0)
    else:
        sent = lax.all_to_all(packed, "ex", split_axis=0, concat_axis=0, tiled=True)
        expert_out = group_sum(group_partial(group_rows(sent))).astype(RETURN_DTYPE)
        mine = lax.all_to_all(expert_out, "ex", split_axis=0, concat_axis=0, tiled=True)
        mine = mine.astype(jnp.float32)
    theirs = shift(mine, "context", n_ctx, 1)
    slots_out = jnp.concatenate([mine, theirs], axis=0).reshape(n_ctx * experts * half, width)

    own_cell = local_cell[:tok]
    expert_of = own_cell // span
    slot_of = own_cell % span
    if experts == 2:
        position = jnp.where(expert_of == me, 0, 1)
    else:
        position = expert_of
    block = jnp.where(slot_of // half == ctx, 0, 1)
    layout = block * (experts * half) + position * half + slot_of % half
    layout = jnp.where(own_cell < experts * span, layout, n_ctx * experts * half)
    own_match = (
        layout[:, :, None] == jnp.arange(n_ctx * experts * half, dtype=jnp.int32)[None, None, :]
    ).astype(jnp.float32)
    mixing = jnp.sum(own_match * route_weight[:, :, None], axis=1)
    mixed = jnp.dot(
        mixing, slots_out, precision=lax.Precision.HIGH, preferred_element_type=jnp.float32
    )
    return mixed.astype(jnp.bfloat16)


def solution(mesh):
    groups, n_expert, n_ctx = mesh.devices.shape
    split = Mesh(
        mesh.devices.reshape(groups, n_expert // SHARERS, SHARERS, n_ctx),
        ("groups", "ex", "sh", "context"),
    )
    rows = P(("groups", "ex", "sh", "context"), None)
    slabs = P(("ex", "sh"), "context", None)
    return jax.shard_map(
        per_device,
        mesh=split,
        in_specs=(rows, rows, rows, slabs, slabs, slabs),
        out_specs=rows,
        check_vma=False,
    )
```

```python
import jax
import jax.numpy as jnp
from jax import lax
from jax.sharding import Mesh
from jax.sharding import PartitionSpec as P

SHARERS = 4
RETURN_DTYPE = jnp.bfloat16


def shift(x, axis, size, k):
    return lax.ppermute(x, axis, [(i, (i + k) % size) for i in range(size)])


def swap(x, axis, size, k):
    return lax.ppermute(x, axis, [(i, i ^ k) for i in range(size)])


def quarter_rows(rows, w_gate, w_up, w_down, n_ctx):
    dims = (((1,), (1,)), ((), ()))
    gate = lax.dot_general(rows, w_gate, dims, preferred_element_type=jnp.float32)
    up = lax.dot_general(rows, w_up, dims, preferred_element_type=jnp.float32)
    hidden = (jax.nn.silu(gate) * up).astype(jnp.bfloat16)
    slab = w_down.shape[0] // n_ctx
    total = None
    for c in range(n_ctx):
        part = jnp.dot(
            hidden[:, c * slab : (c + 1) * slab],
            w_down[c * slab : (c + 1) * slab],
            preferred_element_type=jnp.float32,
        ).astype(jnp.bfloat16)
        total = part.astype(jnp.float32) if total is None else total + part.astype(jnp.float32)
    return total


def per_device(tokens, routes, route_weight, w_gate, w_up, w_down):
    tok = tokens.shape[0]
    top = routes.shape[1]
    width = tokens.shape[1]
    experts = lax.axis_size("ex")
    sharers = lax.axis_size("sh")
    n_ctx = lax.axis_size("context")
    route_count = max(5 * experts, 2 * top)
    capacity = max(2, 5 * tok * top // (2 * route_count))
    half = -(-capacity // n_ctx)
    span = n_ctx * half
    ctx = lax.axis_index("context")
    me = lax.axis_index("ex")

    def with_sibling(x):
        return jnp.concatenate([x, shift(x, "context", n_ctx, 1)], axis=0)

    wg = with_sibling(w_gate[0])
    wu = with_sibling(w_up[0])
    wd = with_sibling(w_down[0])

    other_routes = shift(routes, "context", n_ctx, 1)
    pair_routes = jnp.where(
        ctx == 0,
        jnp.concatenate([routes, other_routes], axis=0),
        jnp.concatenate([other_routes, routes], axis=0),
    )
    ids = jnp.arange(experts, dtype=jnp.int32)
    has = jnp.any(pair_routes[None, :, :] == ids[:, None, None], axis=2).astype(jnp.int32)
    count = jnp.cumsum(has, axis=1) - has
    local_has = jnp.where(ctx == 0, has, jnp.roll(has, tok, axis=1))
    local_slot = jnp.where(ctx == 0, count, jnp.roll(count, tok, axis=1))

    if experts == 2:
        position = jnp.where(ids == me, 0, 1)
        order_has = jnp.where(me == 0, local_has, local_has[::-1])
        order_slot = jnp.where(me == 0, local_slot, local_slot[::-1])
    else:
        position = ids
        order_has, order_slot = local_has, local_slot
    wanted = ctx * half + jnp.arange(half, dtype=jnp.int32)
    picker = (order_has[:, None, :] > 0) & (order_slot[:, None, :] == wanted[None, :, None])
    picker = picker.astype(jnp.bfloat16).reshape(experts * half, n_ctx * tok)
    pair_tokens = with_sibling(tokens)
    packed = jnp.dot(picker, pair_tokens, preferred_element_type=jnp.float32).astype(jnp.bfloat16)
    packed = packed.reshape(experts, half, width)

    def exchange(x, k):
        if sharers & (sharers - 1) == 0:
            return swap(x, "sh", sharers, k)
        return shift(x, "sh", sharers, k)

    def back_exchange(x, k):
        if sharers & (sharers - 1) == 0:
            return swap(x, "sh", sharers, k)
        return shift(x, "sh", sharers, -k)

    def group_partial(sent):
        group = [sent] + [exchange(sent, k) for k in range(1, sharers)]
        rows = jnp.stack(group).reshape(-1, width)
        partial = quarter_rows(rows, wg, wu, wd, n_ctx).astype(jnp.bfloat16)
        return partial.reshape((sharers,) + sent.shape)

    def group_sum(partial):
        total = partial[0].astype(jnp.float32)
        for k in range(1, sharers):
            total = total + back_exchange(partial[k], k).astype(jnp.float32)
        return total

    if experts == 2:
        local_part = group_partial(packed[0:1])
        far_part = group_partial(shift(packed[1:2], "ex", 2, 1))
        far_out = group_sum(far_part)
        local_part, far_out = lax.optimization_barrier((local_part, far_out))
        back = shift(far_out.astype(RETURN_DTYPE), "ex", 2, 1).astype(jnp.float32)
        mine = jnp.concatenate([group_sum(local_part), back], axis=0)
    else:
        sent = lax.all_to_all(packed, "ex", split_axis=0, concat_axis=0, tiled=True)
        expert_out = group_sum(group_partial(sent)).astype(RETURN_DTYPE)
        mine = lax.all_to_all(expert_out, "ex", split_axis=0, concat_axis=0, tiled=True)
        mine = mine.astype(jnp.float32)
    theirs = shift(mine, "context", n_ctx, 1)
    slots_out = jnp.concatenate([mine, theirs], axis=0).reshape(n_ctx * experts * half, width)

    n_slots = n_ctx * experts * half
    own_has = local_has[:, :tok] > 0
    own_slot = local_slot[:, :tok]
    weight = jnp.sum(
        jnp.where(routes[None, :, :] == ids[:, None, None], route_weight[None, :, :], 0.0), axis=2
    )
    block = jnp.where(own_slot // half == ctx, 0, 1)
    layout = block * (experts * half) + position[:, None] * half + own_slot % half
    layout = jnp.where(own_has, layout, n_slots)
    own_match = (layout[:, :, None] == jnp.arange(n_slots, dtype=jnp.int32)[None, None, :]).astype(
        jnp.float32
    )
    mixing = jnp.sum(own_match * weight[:, :, None], axis=0)
    mixed = jnp.dot(
        mixing, slots_out, precision=lax.Precision.HIGH, preferred_element_type=jnp.float32
    )
    return mixed.astype(jnp.bfloat16)


def solution(mesh):
    groups, n_expert, n_ctx = mesh.devices.shape
    split = Mesh(
        mesh.devices.reshape(groups, n_expert // SHARERS, SHARERS, n_ctx),
        ("groups", "ex", "sh", "context"),
    )
    rows = P(("groups", "ex", "sh", "context"), None)
    slabs = P(("ex", "sh"), "context", None)
    return jax.shard_map(
        per_device,
        mesh=split,
        in_specs=(rows, rows, rows, slabs, slabs, slabs),
        out_specs=rows,
        check_vma=False,
    )
```

```python
import jax
import jax.numpy as jnp
from jax import lax
from jax.sharding import Mesh
from jax.sharding import PartitionSpec as P

SHARERS = 4
RETURN_DTYPE = jnp.bfloat16


def shift(x, axis, size, k):
    return lax.ppermute(x, axis, [(i, (i + k) % size) for i in range(size)])


def swap(x, axis, size, k):
    return lax.ppermute(x, axis, [(i, i ^ k) for i in range(size)])


def quarter_rows(rows, w_gate, w_up, w_down, n_ctx):
    dims = (((1,), (1,)), ((), ()))
    gate = lax.dot_general(rows, w_gate, dims, preferred_element_type=jnp.float32)
    up = lax.dot_general(rows, w_up, dims, preferred_element_type=jnp.float32)
    hidden = (jax.nn.silu(gate) * up).astype(jnp.bfloat16)
    slab = w_down.shape[0] // n_ctx
    total = None
    for c in range(n_ctx):
        part = jnp.dot(
            hidden[:, c * slab : (c + 1) * slab],
            w_down[c * slab : (c + 1) * slab],
            preferred_element_type=jnp.float32,
        ).astype(jnp.bfloat16)
        total = part.astype(jnp.float32) if total is None else total + part.astype(jnp.float32)
    return total


def per_device(tokens, routes, route_weight, w_gate, w_up, w_down):
    tok = tokens.shape[0]
    top = routes.shape[1]
    width = tokens.shape[1]
    experts = lax.axis_size("ex")
    sharers = lax.axis_size("sh")
    n_ctx = lax.axis_size("context")
    route_count = max(5 * experts, 2 * top)
    capacity = max(2, 5 * tok * top // (2 * route_count))
    half = -(-capacity // n_ctx)
    span = n_ctx * half
    ctx = lax.axis_index("context")
    me = lax.axis_index("ex")

    def with_sibling(x):
        return jnp.concatenate([x, shift(x, "context", n_ctx, 1)], axis=0)

    wg = with_sibling(w_gate[0])
    wu = with_sibling(w_up[0])
    wd = with_sibling(w_down[0])

    other_routes = shift(routes, "context", n_ctx, 1)
    pair_routes = jnp.where(
        ctx == 0,
        jnp.concatenate([routes, other_routes], axis=0),
        jnp.concatenate([other_routes, routes], axis=0),
    )
    ids = jnp.arange(experts, dtype=jnp.int32)
    has = jnp.any(pair_routes[None, :, :] == ids[:, None, None], axis=2).astype(jnp.int32)
    count = jnp.cumsum(has, axis=1) - has
    local_has = jnp.where(ctx == 0, has, jnp.roll(has, tok, axis=1))
    local_slot = jnp.where(ctx == 0, count, jnp.roll(count, tok, axis=1))

    if experts == 2:
        position = jnp.where(ids == me, 0, 1)
        order_has = jnp.where(me == 0, local_has, local_has[::-1])
        order_slot = jnp.where(me == 0, local_slot, local_slot[::-1])
    else:
        position = ids
        order_has, order_slot = local_has, local_slot
    wanted = ctx * half + jnp.arange(half, dtype=jnp.int32)
    picker = (order_has[:, None, :] > 0) & (order_slot[:, None, :] == wanted[None, :, None])
    picker = lax.optimization_barrier(picker.astype(jnp.bfloat16).reshape(experts * half, n_ctx * tok))
    pair_tokens = with_sibling(tokens)
    packed = jnp.dot(picker, pair_tokens, preferred_element_type=jnp.float32).astype(jnp.bfloat16)
    packed = packed.reshape(experts, half, width)

    def exchange(x, k):
        if sharers & (sharers - 1) == 0:
            return swap(x, "sh", sharers, k)
        return shift(x, "sh", sharers, k)

    def back_exchange(x, k):
        if sharers & (sharers - 1) == 0:
            return swap(x, "sh", sharers, k)
        return shift(x, "sh", sharers, -k)

    def group_partial(sent):
        group = [sent] + [exchange(sent, k) for k in range(1, sharers)]
        rows = jnp.stack(group).reshape(-1, width)
        partial = quarter_rows(rows, wg, wu, wd, n_ctx).astype(jnp.bfloat16)
        return partial.reshape((sharers,) + sent.shape)

    def group_sum(partial):
        total = partial[0].astype(jnp.float32)
        for k in range(1, sharers):
            total = total + back_exchange(partial[k], k).astype(jnp.float32)
        return total

    if experts == 2:
        local_part = group_partial(packed[0:1])
        far_part = group_partial(shift(packed[1:2], "ex", 2, 1))
        far_out = group_sum(far_part)
        local_part, far_out = lax.optimization_barrier((local_part, far_out))
        back = shift(far_out.astype(RETURN_DTYPE), "ex", 2, 1).astype(jnp.float32)
        mine = jnp.concatenate([group_sum(local_part), back], axis=0)
    else:
        sent = lax.all_to_all(packed, "ex", split_axis=0, concat_axis=0, tiled=True)
        expert_out = group_sum(group_partial(sent)).astype(RETURN_DTYPE)
        mine = lax.all_to_all(expert_out, "ex", split_axis=0, concat_axis=0, tiled=True)
        mine = mine.astype(jnp.float32)
    theirs = shift(mine, "context", n_ctx, 1)

    n_slots = n_ctx * experts * half
    own_has = local_has[:, :tok] > 0
    own_slot = local_slot[:, :tok]
    weight = jnp.sum(
        jnp.where(routes[None, :, :] == ids[:, None, None], route_weight[None, :, :], 0.0), axis=2
    )
    block = jnp.where(own_slot // half == ctx, 0, 1)
    layout = block * (experts * half) + position[:, None] * half + own_slot % half
    layout = jnp.where(own_has, layout, n_slots)
    own_match = (layout[:, :, None] == jnp.arange(n_slots, dtype=jnp.int32)[None, None, :]).astype(
        jnp.float32
    )
    mixing = jnp.sum(own_match * weight[:, :, None], axis=0)
    own_rows = experts * half
    dims = (((1,), (0,)), ((), ()))
    mixed = lax.dot_general(
        mixing[:, :own_rows],
        mine.reshape(own_rows, width),
        dims,
        precision=lax.Precision.HIGH,
        preferred_element_type=jnp.float32,
    ) + lax.dot_general(
        mixing[:, own_rows:],
        theirs.reshape(own_rows, width),
        dims,
        precision=lax.Precision.HIGH,
        preferred_element_type=jnp.float32,
    )
    return mixed.astype(jnp.bfloat16)


def solution(mesh):
    groups, n_expert, n_ctx = mesh.devices.shape
    split = Mesh(
        mesh.devices.reshape(groups, n_expert // SHARERS, SHARERS, n_ctx),
        ("groups", "ex", "sh", "context"),
    )
    rows = P(("groups", "ex", "sh", "context"), None)
    slabs = P(("ex", "sh"), "context", None)
    return jax.shard_map(
        per_device,
        mesh=split,
        in_specs=(rows, rows, rows, slabs, slabs, slabs),
        out_specs=rows,
        check_vma=False,
    )
```

```python
import jax
import jax.numpy as jnp
from jax import lax
from jax.sharding import Mesh
from jax.sharding import PartitionSpec as P

SHARERS = 4
RETURN_DTYPE = jnp.bfloat16


def shift(x, axis, size, k):
    return lax.ppermute(x, axis, [(i, (i + k) % size) for i in range(size)])


def swap(x, axis, size, k):
    return lax.ppermute(x, axis, [(i, i ^ k) for i in range(size)])


def quarter_rows(rows, w_gate, w_up, w_down, n_ctx):
    dims = (((1,), (1,)), ((), ()))
    gate = lax.dot_general(rows, w_gate, dims, preferred_element_type=jnp.float32)
    up = lax.dot_general(rows, w_up, dims, preferred_element_type=jnp.float32)
    hidden = (jax.nn.silu(gate) * up).astype(jnp.bfloat16)
    slab = w_down.shape[0] // n_ctx
    total = None
    for c in range(n_ctx):
        part = jnp.dot(
            hidden[:, c * slab : (c + 1) * slab],
            w_down[c * slab : (c + 1) * slab],
            preferred_element_type=jnp.float32,
        ).astype(jnp.bfloat16)
        total = part.astype(jnp.float32) if total is None else total + part.astype(jnp.float32)
    return total


def per_device(tokens, routes, route_weight, w_gate, w_up, w_down):
    tok = tokens.shape[0]
    top = routes.shape[1]
    width = tokens.shape[1]
    experts = lax.axis_size("ex")
    sharers = lax.axis_size("sh")
    n_ctx = lax.axis_size("context")
    route_count = max(5 * experts, 2 * top)
    capacity = max(2, 5 * tok * top // (2 * route_count))
    half = -(-capacity // n_ctx)
    span = n_ctx * half
    ctx = lax.axis_index("context")
    me = lax.axis_index("ex")

    def with_sibling(x):
        return jnp.concatenate([x, shift(x, "context", n_ctx, 1)], axis=0)

    wg = with_sibling(w_gate[0])
    wu = with_sibling(w_up[0])
    wd = with_sibling(w_down[0])

    other_routes = shift(routes, "context", n_ctx, 1)
    pair_routes = jnp.where(
        ctx == 0,
        jnp.concatenate([routes, other_routes], axis=0),
        jnp.concatenate([other_routes, routes], axis=0),
    )
    ids = jnp.arange(experts, dtype=jnp.int32)
    has = jnp.any(pair_routes[None, :, :] == ids[:, None, None], axis=2).astype(jnp.int32)
    count = jnp.cumsum(has, axis=1) - has
    local_has = jnp.where(ctx == 0, has, jnp.roll(has, tok, axis=1))
    local_slot = jnp.where(ctx == 0, count, jnp.roll(count, tok, axis=1))

    if experts == 2:
        position = jnp.where(ids == me, 0, 1)
        order_has = jnp.where(me == 0, local_has, local_has[::-1])
        order_slot = jnp.where(me == 0, local_slot, local_slot[::-1])
    else:
        position = ids
        order_has, order_slot = local_has, local_slot
    wanted = ctx * half + jnp.arange(half, dtype=jnp.int32)
    picker = (order_has[:, None, :] > 0) & (order_slot[:, None, :] == wanted[None, :, None])
    picker = picker.astype(jnp.bfloat16).reshape(experts * half, n_ctx * tok)
    pair_tokens = with_sibling(tokens)
    packed = jnp.dot(picker, pair_tokens, preferred_element_type=jnp.float32).astype(jnp.bfloat16)
    packed = packed.reshape(experts, half, width)

    doubling = sharers & (sharers - 1) == 0

    def group_rows(sent):
        if not doubling:
            return [sent] + [shift(sent, "sh", sharers, k) for k in range(1, sharers)], list(range(sharers))
        blocks, xors = [sent], [0]
        bit = sharers // 2
        while bit:
            recv = swap(jnp.stack(blocks), "sh", sharers, bit)
            blocks = blocks + [recv[i] for i in range(len(blocks))]
            xors = xors + [x ^ bit for x in xors]
            bit //= 2
        return blocks, xors

    def group_partial(gathered):
        blocks, xors = gathered
        rows = jnp.stack(blocks).reshape(-1, width)
        partial = quarter_rows(rows, wg, wu, wd, n_ctx).astype(jnp.bfloat16)
        return partial.reshape((sharers,) + blocks[0].shape), xors

    def group_sum(parts):
        partial, xors = parts
        total = partial[0].astype(jnp.float32)
        for p in range(1, sharers):
            if doubling:
                back_part = swap(partial[p], "sh", sharers, xors[p])
            else:
                back_part = shift(partial[p], "sh", sharers, -xors[p])
            total = total + back_part.astype(jnp.float32)
        return total

    if experts == 2:
        local_part = group_partial(group_rows(packed[0:1]))
        far_part = group_partial(group_rows(shift(packed[1:2], "ex", 2, 1)))
        far_out = group_sum(far_part)
        local_partial, far_out = lax.optimization_barrier((local_part[0], far_out))
        back = shift(far_out.astype(RETURN_DTYPE), "ex", 2, 1).astype(jnp.float32)
        mine = jnp.concatenate([group_sum((local_partial, local_part[1])), back], axis=0)
    else:
        sent = lax.all_to_all(packed, "ex", split_axis=0, concat_axis=0, tiled=True)
        expert_out = group_sum(group_partial(group_rows(sent))).astype(RETURN_DTYPE)
        mine = lax.all_to_all(expert_out, "ex", split_axis=0, concat_axis=0, tiled=True)
        mine = mine.astype(jnp.float32)
    theirs = shift(mine, "context", n_ctx, 1)
    slots_out = jnp.concatenate([mine, theirs], axis=0).reshape(n_ctx * experts * half, width)

    n_slots = n_ctx * experts * half
    own_has = local_has[:, :tok] > 0
    own_slot = local_slot[:, :tok]
    weight = jnp.sum(
        jnp.where(routes[None, :, :] == ids[:, None, None], route_weight[None, :, :], 0.0), axis=2
    )
    block = jnp.where(own_slot // half == ctx, 0, 1)
    layout = block * (experts * half) + position[:, None] * half + own_slot % half
    layout = jnp.where(own_has, layout, n_slots)
    own_match = (layout[:, :, None] == jnp.arange(n_slots, dtype=jnp.int32)[None, None, :]).astype(
        jnp.float32
    )
    mixing = jnp.sum(own_match * weight[:, :, None], axis=0)
    mixed = jnp.dot(
        mixing, slots_out, precision=lax.Precision.HIGH, preferred_element_type=jnp.float32
    )
    return mixed.astype(jnp.bfloat16)


def solution(mesh):
    groups, n_expert, n_ctx = mesh.devices.shape
    split = Mesh(
        mesh.devices.reshape(groups, n_expert // SHARERS, SHARERS, n_ctx),
        ("groups", "ex", "sh", "context"),
    )
    rows = P(("groups", "ex", "sh", "context"), None)
    slabs = P(("ex", "sh"), "context", None)
    return jax.shard_map(
        per_device,
        mesh=split,
        in_specs=(rows, rows, rows, slabs, slabs, slabs),
        out_specs=rows,
        check_vma=False,
    )
```

```python
import jax
import jax.numpy as jnp
from jax import lax
from jax.sharding import Mesh
from jax.sharding import PartitionSpec as P

SHARERS = 4
RETURN_DTYPE = jnp.bfloat16


def shift(x, axis, size, k):
    return lax.ppermute(x, axis, [(i, (i + k) % size) for i in range(size)])


def swap(x, axis, size, k):
    return lax.ppermute(x, axis, [(i, i ^ k) for i in range(size)])


def quarter_rows(rows, w_gate, w_up, w_down, n_ctx):
    dims = (((1,), (1,)), ((), ()))
    gate = lax.dot_general(rows, w_gate, dims, preferred_element_type=jnp.float32)
    up = lax.dot_general(rows, w_up, dims, preferred_element_type=jnp.float32)
    hidden = (jax.nn.silu(gate) * up).astype(jnp.bfloat16)
    slab = w_down.shape[0] // n_ctx
    total = None
    for c in range(n_ctx):
        part = jnp.dot(
            hidden[:, c * slab : (c + 1) * slab],
            w_down[c * slab : (c + 1) * slab],
            preferred_element_type=jnp.float32,
        ).astype(jnp.bfloat16)
        total = part.astype(jnp.float32) if total is None else total + part.astype(jnp.float32)
    return total


def per_device(tokens, routes, route_weight, w_gate, w_up, w_down):
    tok = tokens.shape[0]
    top = routes.shape[1]
    width = tokens.shape[1]
    experts = lax.axis_size("ex")
    sharers = lax.axis_size("sh")
    n_ctx = lax.axis_size("context")
    route_count = max(5 * experts, 2 * top)
    capacity = max(2, 5 * tok * top // (2 * route_count))
    half = -(-capacity // n_ctx)
    span = n_ctx * half
    ctx = lax.axis_index("context")
    me = lax.axis_index("ex")

    def with_sibling(x):
        return jnp.concatenate([x, shift(x, "context", n_ctx, 1)], axis=0)

    wg = with_sibling(w_gate[0])
    wu = with_sibling(w_up[0])
    wd = with_sibling(w_down[0])

    other_routes = shift(routes, "context", n_ctx, 1)
    pair_routes = jnp.where(
        ctx == 0,
        jnp.concatenate([routes, other_routes], axis=0),
        jnp.concatenate([other_routes, routes], axis=0),
    )
    ids = jnp.arange(experts, dtype=jnp.int32)
    has = jnp.any(pair_routes[None, :, :] == ids[:, None, None], axis=2).astype(jnp.int32)
    count = jnp.cumsum(has, axis=1) - has
    local_has = jnp.where(ctx == 0, has, jnp.roll(has, tok, axis=1))
    local_slot = jnp.where(ctx == 0, count, jnp.roll(count, tok, axis=1))

    if experts == 2:
        position = jnp.where(ids == me, 0, 1)
        order_has = jnp.where(me == 0, local_has, local_has[::-1])
        order_slot = jnp.where(me == 0, local_slot, local_slot[::-1])
    else:
        position = ids
        order_has, order_slot = local_has, local_slot
    wanted = ctx * half + jnp.arange(half, dtype=jnp.int32)
    picker = (order_has[:, None, :] > 0) & (order_slot[:, None, :] == wanted[None, :, None])
    picker = picker.astype(jnp.bfloat16).reshape(experts * half, n_ctx * tok)
    pair_tokens = with_sibling(tokens)
    packed = jnp.dot(picker, pair_tokens, preferred_element_type=jnp.float32).astype(jnp.bfloat16)
    packed = packed.reshape(experts, half, width)

    def exchange(x, k):
        if sharers & (sharers - 1) == 0:
            return swap(x, "sh", sharers, k)
        return shift(x, "sh", sharers, k)

    def back_exchange(x, k):
        if sharers & (sharers - 1) == 0:
            return swap(x, "sh", sharers, k)
        return shift(x, "sh", sharers, -k)

    def group_partial(sent):
        group = [sent] + [exchange(sent, k) for k in range(1, sharers)]
        rows = jnp.stack(group).reshape(-1, width)
        partial = quarter_rows(rows, wg, wu, wd, n_ctx).astype(jnp.bfloat16)
        return partial.reshape((sharers,) + sent.shape)

    def group_sum(partial):
        total = partial[0].astype(jnp.float32)
        for k in range(1, sharers):
            total = total + back_exchange(partial[k], k).astype(jnp.float32)
        return total

    if experts == 2:
        local_part = group_partial(packed[0:1])
        far_part = group_partial(shift(packed[1:2], "ex", 2, 1))
        far_out = group_sum(far_part)
        back = shift(far_out.astype(RETURN_DTYPE), "ex", 2, 1).astype(jnp.float32)
        mine = jnp.concatenate([group_sum(local_part), back], axis=0)
    else:
        sent = lax.all_to_all(packed, "ex", split_axis=0, concat_axis=0, tiled=True)
        expert_out = group_sum(group_partial(sent)).astype(RETURN_DTYPE)
        mine = lax.all_to_all(expert_out, "ex", split_axis=0, concat_axis=0, tiled=True)
        mine = mine.astype(jnp.float32)
    theirs = shift(mine, "context", n_ctx, 1)
    slots_out = jnp.concatenate([mine, theirs], axis=0).reshape(n_ctx * experts * half, width)

    n_slots = n_ctx * experts * half
    own_has = local_has[:, :tok] > 0
    own_slot = local_slot[:, :tok]
    weight = jnp.sum(
        jnp.where(routes[None, :, :] == ids[:, None, None], route_weight[None, :, :], 0.0), axis=2
    )
    block = jnp.where(own_slot // half == ctx, 0, 1)
    layout = block * (experts * half) + position[:, None] * half + own_slot % half
    layout = jnp.where(own_has, layout, n_slots)
    own_match = (layout[:, :, None] == jnp.arange(n_slots, dtype=jnp.int32)[None, None, :]).astype(
        jnp.float32
    )
    mixing = jnp.sum(own_match * weight[:, :, None], axis=0)
    mixed = jnp.dot(
        mixing, slots_out, precision=lax.Precision.HIGH, preferred_element_type=jnp.float32
    )
    return mixed.astype(jnp.bfloat16)


def solution(mesh):
    groups, n_expert, n_ctx = mesh.devices.shape
    split = Mesh(
        mesh.devices.reshape(groups, n_expert // SHARERS, SHARERS, n_ctx),
        ("groups", "ex", "sh", "context"),
    )
    rows = P(("groups", "ex", "sh", "context"), None)
    slabs = P(("ex", "sh"), "context", None)
    return jax.shard_map(
        per_device,
        mesh=split,
        in_specs=(rows, rows, rows, slabs, slabs, slabs),
        out_specs=rows,
        check_vma=False,
    )
```

```python
import jax
import jax.numpy as jnp
from jax import lax
from jax.sharding import Mesh
from jax.sharding import PartitionSpec as P

SHARERS = 4
RETURN_DTYPE = jnp.bfloat16


def shift(x, axis, size, k):
    return lax.ppermute(x, axis, [(i, (i + k) % size) for i in range(size)])


def swap(x, axis, size, k):
    return lax.ppermute(x, axis, [(i, i ^ k) for i in range(size)])


def quarter_rows(rows, w_gate, w_up, w_down, n_ctx):
    dims = (((1,), (1,)), ((), ()))
    gate = lax.dot_general(rows, w_gate, dims, preferred_element_type=jnp.float32)
    up = lax.dot_general(rows, w_up, dims, preferred_element_type=jnp.float32)
    hidden = (jax.nn.silu(gate) * up).astype(jnp.bfloat16)
    slab = w_down.shape[0] // n_ctx
    total = None
    for c in range(n_ctx):
        part = jnp.dot(
            hidden[:, c * slab : (c + 1) * slab],
            w_down[c * slab : (c + 1) * slab],
            preferred_element_type=jnp.float32,
        ).astype(jnp.bfloat16)
        total = part.astype(jnp.float32) if total is None else total + part.astype(jnp.float32)
    return total


def per_device(tokens, routes, route_weight, w_gate, w_up, w_down):
    tok = tokens.shape[0]
    top = routes.shape[1]
    width = tokens.shape[1]
    experts = lax.axis_size("ex")
    sharers = lax.axis_size("sh")
    n_ctx = lax.axis_size("context")
    route_count = max(5 * experts, 2 * top)
    capacity = max(2, 5 * tok * top // (2 * route_count))
    half = -(-capacity // n_ctx)
    span = n_ctx * half
    ctx = lax.axis_index("context")
    me = lax.axis_index("ex")

    def with_sibling(x):
        return jnp.concatenate([x, shift(x, "context", n_ctx, 1)], axis=0)

    wg = with_sibling(w_gate[0])
    wu = with_sibling(w_up[0])
    wd = with_sibling(w_down[0])

    other_routes = shift(routes, "context", n_ctx, 1)
    pair_routes = jnp.where(
        ctx == 0,
        jnp.concatenate([routes, other_routes], axis=0),
        jnp.concatenate([other_routes, routes], axis=0),
    )
    ids = jnp.arange(experts, dtype=jnp.int32)
    has = jnp.any(pair_routes[None, :, :] == ids[:, None, None], axis=2).astype(jnp.int32)
    count = jnp.cumsum(has, axis=1) - has
    local_has = jnp.where(ctx == 0, has, jnp.roll(has, tok, axis=1))
    local_slot = jnp.where(ctx == 0, count, jnp.roll(count, tok, axis=1))

    if experts == 2:
        position = jnp.where(ids == me, 0, 1)
        order_has = jnp.where(me == 0, local_has, local_has[::-1])
        order_slot = jnp.where(me == 0, local_slot, local_slot[::-1])
    else:
        position = ids
        order_has, order_slot = local_has, local_slot
    wanted = ctx * half + jnp.arange(half, dtype=jnp.int32)
    picker = (order_has[:, None, :] > 0) & (order_slot[:, None, :] == wanted[None, :, None])
    picker = picker.astype(jnp.bfloat16).reshape(experts * half, n_ctx * tok)
    pair_tokens = with_sibling(tokens)
    packed = jnp.dot(picker, pair_tokens, preferred_element_type=jnp.float32).astype(jnp.bfloat16)
    packed = packed.reshape(experts, half, width)

    def exchange(x, k):
        if sharers & (sharers - 1) == 0:
            return swap(x, "sh", sharers, k)
        return shift(x, "sh", sharers, k)

    def back_exchange(x, k):
        if sharers & (sharers - 1) == 0:
            return swap(x, "sh", sharers, k)
        return shift(x, "sh", sharers, -k)

    def group_partial(sent):
        group = [sent] + [exchange(sent, k) for k in range(1, sharers)]
        rows = jnp.stack(group).reshape(-1, width)
        partial = quarter_rows(rows, wg, wu, wd, n_ctx).astype(jnp.bfloat16)
        return partial.reshape((sharers,) + sent.shape)

    def group_sum(partial):
        total = partial[0].astype(jnp.float32)
        for k in range(1, sharers):
            total = total + back_exchange(partial[k], k).astype(jnp.float32)
        return total

    if experts == 2:
        local_part = group_partial(packed[0:1])
        far_part = group_partial(shift(packed[1:2], "ex", 2, 1))
        far_out = group_sum(far_part)
        back = shift(far_out.astype(RETURN_DTYPE), "ex", 2, 1)
        local_out = group_sum(local_part)
        mine = jnp.concatenate([local_out, back.astype(jnp.float32)], axis=0)
        theirs = jnp.concatenate(
            [shift(local_out, "context", n_ctx, 1), shift(back, "context", n_ctx, 1).astype(jnp.float32)],
            axis=0,
        )
    else:
        sent = lax.all_to_all(packed, "ex", split_axis=0, concat_axis=0, tiled=True)
        expert_out = group_sum(group_partial(sent)).astype(RETURN_DTYPE)
        mine = lax.all_to_all(expert_out, "ex", split_axis=0, concat_axis=0, tiled=True)
        mine = mine.astype(jnp.float32)
        theirs = shift(mine, "context", n_ctx, 1)

    n_slots = n_ctx * experts * half
    own_has = local_has[:, :tok] > 0
    own_slot = local_slot[:, :tok]
    weight = jnp.sum(
        jnp.where(routes[None, :, :] == ids[:, None, None], route_weight[None, :, :], 0.0), axis=2
    )
    block = jnp.where(own_slot // half == ctx, 0, 1)
    layout = block * (experts * half) + position[:, None] * half + own_slot % half
    layout = jnp.where(own_has, layout, n_slots)
    own_match = (layout[:, :, None] == jnp.arange(n_slots, dtype=jnp.int32)[None, None, :]).astype(
        jnp.float32
    )
    mixing = jnp.sum(own_match * weight[:, :, None], axis=0)
    own_rows = experts * half
    dims = (((1,), (0,)), ((), ()))
    mixed = lax.dot_general(
        mixing[:, :own_rows],
        mine.reshape(own_rows, width),
        dims,
        precision=lax.Precision.HIGH,
        preferred_element_type=jnp.float32,
    ) + lax.dot_general(
        mixing[:, own_rows:],
        theirs.reshape(own_rows, width),
        dims,
        precision=lax.Precision.HIGH,
        preferred_element_type=jnp.float32,
    )
    return mixed.astype(jnp.bfloat16)


def solution(mesh):
    groups, n_expert, n_ctx = mesh.devices.shape
    split = Mesh(
        mesh.devices.reshape(groups, n_expert // SHARERS, SHARERS, n_ctx),
        ("groups", "ex", "sh", "context"),
    )
    rows = P(("groups", "ex", "sh", "context"), None)
    slabs = P(("ex", "sh"), "context", None)
    return jax.shard_map(
        per_device,
        mesh=split,
        in_specs=(rows, rows, rows, slabs, slabs, slabs),
        out_specs=rows,
        check_vma=False,
    )
```

```python
import jax
import jax.numpy as jnp
from jax import lax
from jax.sharding import Mesh
from jax.sharding import PartitionSpec as P

SHARERS = 4
RETURN_DTYPE = jnp.bfloat16


def shift(x, axis, size, k):
    return lax.ppermute(x, axis, [(i, (i + k) % size) for i in range(size)])


def swap(x, axis, size, k):
    return lax.ppermute(x, axis, [(i, i ^ k) for i in range(size)])


def quarter_rows(rows, w_gate, w_up, w_down, n_ctx):
    dims = (((1,), (1,)), ((), ()))
    gate = lax.dot_general(rows, w_gate, dims, preferred_element_type=jnp.float32)
    up = lax.dot_general(rows, w_up, dims, preferred_element_type=jnp.float32)
    hidden = (jax.nn.silu(gate) * up).astype(jnp.bfloat16)
    slab = w_down.shape[0] // n_ctx
    total = None
    for c in range(n_ctx):
        part = jnp.dot(
            hidden[:, c * slab : (c + 1) * slab],
            w_down[c * slab : (c + 1) * slab],
            preferred_element_type=jnp.float32,
        ).astype(jnp.bfloat16)
        total = part.astype(jnp.float32) if total is None else total + part.astype(jnp.float32)
    return total


def per_device(tokens, routes, route_weight, w_gate, w_up, w_down):
    tok = tokens.shape[0]
    top = routes.shape[1]
    width = tokens.shape[1]
    experts = lax.axis_size("ex")
    sharers = lax.axis_size("sh")
    n_ctx = lax.axis_size("context")
    route_count = max(5 * experts, 2 * top)
    capacity = max(2, 5 * tok * top // (2 * route_count))
    half = -(-capacity // n_ctx)
    span = n_ctx * half
    ctx = lax.axis_index("context")
    me = lax.axis_index("ex")

    def with_sibling(x):
        return jnp.concatenate([x, shift(x, "context", n_ctx, 1)], axis=0)

    wg = with_sibling(w_gate[0])
    wu = with_sibling(w_up[0])
    wd_other = shift(w_down[0], "context", n_ctx, 1)

    other_routes = shift(routes, "context", n_ctx, 1)
    pair_routes = jnp.where(
        ctx == 0,
        jnp.concatenate([routes, other_routes], axis=0),
        jnp.concatenate([other_routes, routes], axis=0),
    )
    ids = jnp.arange(experts, dtype=jnp.int32)
    has = jnp.any(pair_routes[None, :, :] == ids[:, None, None], axis=2).astype(jnp.int32)
    count = jnp.cumsum(has, axis=1) - has
    local_has = jnp.where(ctx == 0, has, jnp.roll(has, tok, axis=1))
    local_slot = jnp.where(ctx == 0, count, jnp.roll(count, tok, axis=1))

    if experts == 2:
        position = jnp.where(ids == me, 0, 1)
        order_has = jnp.where(me == 0, local_has, local_has[::-1])
        order_slot = jnp.where(me == 0, local_slot, local_slot[::-1])
    else:
        position = ids
        order_has, order_slot = local_has, local_slot
    wanted = ctx * half + jnp.arange(half, dtype=jnp.int32)
    picker = (order_has[:, None, :] > 0) & (order_slot[:, None, :] == wanted[None, :, None])
    picker = picker.astype(jnp.bfloat16).reshape(experts * half, n_ctx * tok)
    pair_tokens = with_sibling(tokens)
    packed = jnp.dot(picker, pair_tokens, preferred_element_type=jnp.float32).astype(jnp.bfloat16)
    packed = packed.reshape(experts, half, width)

    def exchange(x, k):
        if sharers & (sharers - 1) == 0:
            return swap(x, "sh", sharers, k)
        return shift(x, "sh", sharers, k)

    def back_exchange(x, k):
        if sharers & (sharers - 1) == 0:
            return swap(x, "sh", sharers, k)
        return shift(x, "sh", sharers, -k)

    def group_partial(sent, wd):
        group = [sent] + [exchange(sent, k) for k in range(1, sharers)]
        rows = jnp.stack(group).reshape(-1, width)
        partial = quarter_rows(rows, wg, wu, wd, n_ctx).astype(jnp.bfloat16)
        return partial.reshape((sharers,) + sent.shape)

    def group_sum(partial):
        total = partial[0].astype(jnp.float32)
        for k in range(1, sharers):
            total = total + back_exchange(partial[k], k).astype(jnp.float32)
        return total

    if experts == 2:
        far_sent, wd_other = lax.optimization_barrier((shift(packed[1:2], "ex", 2, 1), wd_other))
        wd = jnp.concatenate([w_down[0], wd_other], axis=0)
        local_part = group_partial(packed[0:1], wd)
        far_part = group_partial(far_sent, wd)
        far_out = group_sum(far_part)
        back = shift(far_out.astype(RETURN_DTYPE), "ex", 2, 1).astype(jnp.float32)
        mine = jnp.concatenate([group_sum(local_part), back], axis=0)
    else:
        sent = lax.all_to_all(packed, "ex", split_axis=0, concat_axis=0, tiled=True)
        wd = jnp.concatenate([w_down[0], wd_other], axis=0)
        expert_out = group_sum(group_partial(sent, wd)).astype(RETURN_DTYPE)
        mine = lax.all_to_all(expert_out, "ex", split_axis=0, concat_axis=0, tiled=True)
        mine = mine.astype(jnp.float32)
    theirs = shift(mine, "context", n_ctx, 1)
    slots_out = jnp.concatenate([mine, theirs], axis=0).reshape(n_ctx * experts * half, width)

    n_slots = n_ctx * experts * half
    own_has = local_has[:, :tok] > 0
    own_slot = local_slot[:, :tok]
    weight = jnp.sum(
        jnp.where(routes[None, :, :] == ids[:, None, None], route_weight[None, :, :], 0.0), axis=2
    )
    block = jnp.where(own_slot // half == ctx, 0, 1)
    layout = block * (experts * half) + position[:, None] * half + own_slot % half
    layout = jnp.where(own_has, layout, n_slots)
    own_match = (layout[:, :, None] == jnp.arange(n_slots, dtype=jnp.int32)[None, None, :]).astype(
        jnp.float32
    )
    mixing = jnp.sum(own_match * weight[:, :, None], axis=0)
    mixed = jnp.dot(
        mixing, slots_out, precision=lax.Precision.HIGH, preferred_element_type=jnp.float32
    )
    return mixed.astype(jnp.bfloat16)


def solution(mesh):
    groups, n_expert, n_ctx = mesh.devices.shape
    split = Mesh(
        mesh.devices.reshape(groups, n_expert // SHARERS, SHARERS, n_ctx),
        ("groups", "ex", "sh", "context"),
    )
    rows = P(("groups", "ex", "sh", "context"), None)
    slabs = P(("ex", "sh"), "context", None)
    return jax.shard_map(
        per_device,
        mesh=split,
        in_specs=(rows, rows, rows, slabs, slabs, slabs),
        out_specs=rows,
        check_vma=False,
    )
```

```python
import jax
import jax.numpy as jnp
from jax import lax
from jax.sharding import Mesh
from jax.sharding import PartitionSpec as P

SHARERS = 4
RETURN_DTYPE = jnp.bfloat16


def shift(x, axis, size, k):
    return lax.ppermute(x, axis, [(i, (i + k) % size) for i in range(size)])


def swap(x, axis, size, k):
    return lax.ppermute(x, axis, [(i, i ^ k) for i in range(size)])


def quarter_rows(rows, w_gate, w_up, w_down, n_ctx):
    dims = (((1,), (1,)), ((), ()))
    gate = lax.dot_general(rows, w_gate, dims, preferred_element_type=jnp.float32)
    up = lax.dot_general(rows, w_up, dims, preferred_element_type=jnp.float32)
    hidden = (jax.nn.silu(gate) * up).astype(jnp.bfloat16)
    slab = w_down.shape[0] // n_ctx
    total = None
    for c in range(n_ctx):
        part = jnp.dot(
            hidden[:, c * slab : (c + 1) * slab],
            w_down[c * slab : (c + 1) * slab],
            preferred_element_type=jnp.float32,
        ).astype(jnp.bfloat16)
        total = part.astype(jnp.float32) if total is None else total + part.astype(jnp.float32)
    return total


def per_device(tokens, routes, route_weight, w_gate, w_up, w_down):
    tok = tokens.shape[0]
    top = routes.shape[1]
    width = tokens.shape[1]
    experts = lax.axis_size("ex")
    sharers = lax.axis_size("sh")
    n_ctx = lax.axis_size("context")
    route_count = max(5 * experts, 2 * top)
    capacity = max(2, 5 * tok * top // (2 * route_count))
    half = -(-capacity // n_ctx)
    span = n_ctx * half
    ctx = lax.axis_index("context")
    me = lax.axis_index("ex")

    def with_sibling(x):
        return jnp.concatenate([x, shift(x, "context", n_ctx, 1)], axis=0)

    wg = with_sibling(w_gate[0])
    wu = with_sibling(w_up[0])
    wd = with_sibling(w_down[0])

    other_routes = shift(routes, "context", n_ctx, 1)
    pair_routes = jnp.where(
        ctx == 0,
        jnp.concatenate([routes, other_routes], axis=0),
        jnp.concatenate([other_routes, routes], axis=0),
    )
    ids = jnp.arange(experts, dtype=jnp.int32)
    has = jnp.any(pair_routes[None, :, :] == ids[:, None, None], axis=2).astype(jnp.int32)
    count = jnp.cumsum(has, axis=1) - has
    local_has = jnp.where(ctx == 0, has, jnp.roll(has, tok, axis=1))
    local_slot = jnp.where(ctx == 0, count, jnp.roll(count, tok, axis=1))

    if experts == 2:
        position = jnp.where(ids == me, 0, 1)
        order_has = jnp.where(me == 0, local_has, local_has[::-1])
        order_slot = jnp.where(me == 0, local_slot, local_slot[::-1])
    else:
        position = ids
        order_has, order_slot = local_has, local_slot
    wanted = ctx * half + jnp.arange(half, dtype=jnp.int32)
    picker = (order_has[:, None, :] > 0) & (order_slot[:, None, :] == wanted[None, :, None])
    picker = picker.astype(jnp.bfloat16).reshape(experts * half, n_ctx * tok)
    pair_tokens = with_sibling(tokens)
    packed = jnp.dot(picker, pair_tokens, preferred_element_type=jnp.float32).astype(jnp.bfloat16)
    packed = packed.reshape(experts, half, width)

    def exchange(x, k):
        if sharers & (sharers - 1) == 0:
            return swap(x, "sh", sharers, k)
        return shift(x, "sh", sharers, k)

    def back_exchange(x, k):
        if sharers & (sharers - 1) == 0:
            return swap(x, "sh", sharers, k)
        return shift(x, "sh", sharers, -k)

    def group_partial(sent):
        order = list(range(sharers - 1, 0, -1))
        received = {k: exchange(sent, k) for k in order}
        group = [sent] + [received[k] for k in range(1, sharers)]
        rows = jnp.stack(group).reshape(-1, width)
        partial = quarter_rows(rows, wg, wu, wd, n_ctx).astype(jnp.bfloat16)
        return partial.reshape((sharers,) + sent.shape)

    def group_sum(partial):
        total = partial[0].astype(jnp.float32)
        for k in range(sharers - 1, 0, -1):
            total = total + back_exchange(partial[k], k).astype(jnp.float32)
        return total

    if experts == 2:
        local_part = group_partial(packed[0:1])
        far_part = group_partial(shift(packed[1:2], "ex", 2, 1))
        far_out = group_sum(far_part)
        back = shift(far_out.astype(RETURN_DTYPE), "ex", 2, 1).astype(jnp.float32)
        mine = jnp.concatenate([group_sum(local_part), back], axis=0)
    else:
        sent = lax.all_to_all(packed, "ex", split_axis=0, concat_axis=0, tiled=True)
        expert_out = group_sum(group_partial(sent)).astype(RETURN_DTYPE)
        mine = lax.all_to_all(expert_out, "ex", split_axis=0, concat_axis=0, tiled=True)
        mine = mine.astype(jnp.float32)
    theirs = shift(mine, "context", n_ctx, 1)
    slots_out = jnp.concatenate([mine, theirs], axis=0).reshape(n_ctx * experts * half, width)

    n_slots = n_ctx * experts * half
    own_has = local_has[:, :tok] > 0
    own_slot = local_slot[:, :tok]
    weight = jnp.sum(
        jnp.where(routes[None, :, :] == ids[:, None, None], route_weight[None, :, :], 0.0), axis=2
    )
    block = jnp.where(own_slot // half == ctx, 0, 1)
    layout = block * (experts * half) + position[:, None] * half + own_slot % half
    layout = jnp.where(own_has, layout, n_slots)
    own_match = (layout[:, :, None] == jnp.arange(n_slots, dtype=jnp.int32)[None, None, :]).astype(
        jnp.float32
    )
    mixing = jnp.sum(own_match * weight[:, :, None], axis=0)
    mixed = jnp.dot(
        mixing, slots_out, precision=lax.Precision.HIGH, preferred_element_type=jnp.float32
    )
    return mixed.astype(jnp.bfloat16)


def solution(mesh):
    groups, n_expert, n_ctx = mesh.devices.shape
    split = Mesh(
        mesh.devices.reshape(groups, n_expert // SHARERS, SHARERS, n_ctx),
        ("groups", "ex", "sh", "context"),
    )
    rows = P(("groups", "ex", "sh", "context"), None)
    slabs = P(("ex", "sh"), "context", None)
    return jax.shard_map(
        per_device,
        mesh=split,
        in_specs=(rows, rows, rows, slabs, slabs, slabs),
        out_specs=rows,
        check_vma=False,
    )
```

```python
import jax
import jax.numpy as jnp
from jax import lax
from jax.sharding import Mesh
from jax.sharding import PartitionSpec as P

SHARERS = 4
RETURN_DTYPE = jnp.bfloat16


def shift(x, axis, size, k):
    return lax.ppermute(x, axis, [(i, (i + k) % size) for i in range(size)])


def swap(x, axis, size, k):
    return lax.ppermute(x, axis, [(i, i ^ k) for i in range(size)])


def quarter_rows(rows, w_gate, w_up, w_down, n_ctx):
    dims = (((1,), (1,)), ((), ()))
    gate = lax.dot_general(rows, w_gate, dims, preferred_element_type=jnp.float32)
    up = lax.dot_general(rows, w_up, dims, preferred_element_type=jnp.float32)
    hidden = (jax.nn.silu(gate) * up).astype(jnp.bfloat16)
    slab = w_down.shape[0] // n_ctx
    total = None
    for c in range(n_ctx):
        part = jnp.dot(
            hidden[:, c * slab : (c + 1) * slab],
            w_down[c * slab : (c + 1) * slab],
            preferred_element_type=jnp.float32,
        ).astype(jnp.bfloat16)
        total = part.astype(jnp.float32) if total is None else total + part.astype(jnp.float32)
    return total


def per_device(tokens, routes, route_weight, w_gate, w_up, w_down):
    tok = tokens.shape[0]
    top = routes.shape[1]
    width = tokens.shape[1]
    experts = lax.axis_size("ex")
    sharers = lax.axis_size("sh")
    n_ctx = lax.axis_size("context")
    route_count = max(5 * experts, 2 * top)
    capacity = max(2, 5 * tok * top // (2 * route_count))
    half = -(-capacity // n_ctx)
    span = n_ctx * half
    ctx = lax.axis_index("context")
    me = lax.axis_index("ex")

    def with_sibling(x):
        return jnp.concatenate([x, shift(x, "context", n_ctx, 1)], axis=0)

    wg = with_sibling(w_gate[0])
    wu = with_sibling(w_up[0])
    wd = with_sibling(w_down[0])

    other_routes = shift(routes, "context", n_ctx, 1)
    pair_routes = jnp.where(
        ctx == 0,
        jnp.concatenate([routes, other_routes], axis=0),
        jnp.concatenate([other_routes, routes], axis=0),
    )
    ids = jnp.arange(experts, dtype=jnp.int32)
    has = jnp.any(pair_routes[None, :, :] == ids[:, None, None], axis=2).astype(jnp.int32)
    count = jnp.cumsum(has, axis=1) - has
    local_has = jnp.where(ctx == 0, has, jnp.roll(has, tok, axis=1))
    local_slot = jnp.where(ctx == 0, count, jnp.roll(count, tok, axis=1))

    if experts == 2:
        position = jnp.where(ids == me, 0, 1)
        order_has = jnp.where(me == 0, local_has, local_has[::-1])
        order_slot = jnp.where(me == 0, local_slot, local_slot[::-1])
    else:
        position = ids
        order_has, order_slot = local_has, local_slot
    wanted = ctx * half + jnp.arange(half, dtype=jnp.int32)
    picker = (order_has[:, None, :] > 0) & (order_slot[:, None, :] == wanted[None, :, None])
    picker = picker.astype(jnp.bfloat16).reshape(experts * half, n_ctx * tok)
    pair_tokens = with_sibling(tokens)
    packed = jnp.dot(picker, pair_tokens, preferred_element_type=jnp.float32).astype(jnp.bfloat16)
    packed = packed.reshape(experts, half, width)

    def exchange(x, k):
        if sharers & (sharers - 1) == 0:
            return swap(x, "sh", sharers, k)
        return shift(x, "sh", sharers, k)

    def back_exchange(x, k):
        if sharers & (sharers - 1) == 0:
            return swap(x, "sh", sharers, k)
        return shift(x, "sh", sharers, -k)

    def group_partial(sent):
        order = list(range(sharers - 1, 0, -1))
        received = {k: exchange(sent, k) for k in order}
        group = [sent] + [received[k] for k in range(1, sharers)]
        rows = jnp.stack(group).reshape(-1, width)
        partial = quarter_rows(rows, wg, wu, wd, n_ctx).astype(jnp.bfloat16)
        return partial.reshape((sharers,) + sent.shape)

    def group_sum(partial, far_first=True):
        total = partial[0].astype(jnp.float32)
        for k in range(sharers - 1, 0, -1) if far_first else range(1, sharers):
            total = total + back_exchange(partial[k], k).astype(jnp.float32)
        return total

    if experts == 2:
        local_part = group_partial(packed[0:1])
        far_part = group_partial(shift(packed[1:2], "ex", 2, 1))
        far_out = group_sum(far_part)
        back = shift(far_out.astype(RETURN_DTYPE), "ex", 2, 1).astype(jnp.float32)
        mine = jnp.concatenate([group_sum(local_part, far_first=False), back], axis=0)
    else:
        sent = lax.all_to_all(packed, "ex", split_axis=0, concat_axis=0, tiled=True)
        expert_out = group_sum(group_partial(sent)).astype(RETURN_DTYPE)
        mine = lax.all_to_all(expert_out, "ex", split_axis=0, concat_axis=0, tiled=True)
        mine = mine.astype(jnp.float32)
    theirs = shift(mine, "context", n_ctx, 1)
    slots_out = jnp.concatenate([mine, theirs], axis=0).reshape(n_ctx * experts * half, width)

    n_slots = n_ctx * experts * half
    own_has = local_has[:, :tok] > 0
    own_slot = local_slot[:, :tok]
    weight = jnp.sum(
        jnp.where(routes[None, :, :] == ids[:, None, None], route_weight[None, :, :], 0.0), axis=2
    )
    block = jnp.where(own_slot // half == ctx, 0, 1)
    layout = block * (experts * half) + position[:, None] * half + own_slot % half
    layout = jnp.where(own_has, layout, n_slots)
    own_match = (layout[:, :, None] == jnp.arange(n_slots, dtype=jnp.int32)[None, None, :]).astype(
        jnp.float32
    )
    mixing = jnp.sum(own_match * weight[:, :, None], axis=0)
    mixed = jnp.dot(
        mixing, slots_out, precision=lax.Precision.HIGH, preferred_element_type=jnp.float32
    )
    return mixed.astype(jnp.bfloat16)


def solution(mesh):
    groups, n_expert, n_ctx = mesh.devices.shape
    split = Mesh(
        mesh.devices.reshape(groups, n_expert // SHARERS, SHARERS, n_ctx),
        ("groups", "ex", "sh", "context"),
    )
    rows = P(("groups", "ex", "sh", "context"), None)
    slabs = P(("ex", "sh"), "context", None)
    return jax.shard_map(
        per_device,
        mesh=split,
        in_specs=(rows, rows, rows, slabs, slabs, slabs),
        out_specs=rows,
        check_vma=False,
    )
```

```python
import jax
import jax.numpy as jnp
from jax import lax
from jax.sharding import Mesh
from jax.sharding import PartitionSpec as P

SHARERS = 4
RETURN_DTYPE = jnp.bfloat16


def shift(x, axis, size, k):
    return lax.ppermute(x, axis, [(i, (i + k) % size) for i in range(size)])


def swap(x, axis, size, k):
    return lax.ppermute(x, axis, [(i, i ^ k) for i in range(size)])


def quarter_rows(rows, w_gate, w_up, w_down, n_ctx):
    dims = (((1,), (1,)), ((), ()))
    gate = lax.dot_general(rows, w_gate, dims, preferred_element_type=jnp.float32)
    up = lax.dot_general(rows, w_up, dims, preferred_element_type=jnp.float32)
    hidden = (jax.nn.silu(gate) * up).astype(jnp.bfloat16)
    slab = w_down.shape[0] // n_ctx
    total = None
    for c in range(n_ctx):
        part = jnp.dot(
            hidden[:, c * slab : (c + 1) * slab],
            w_down[c * slab : (c + 1) * slab],
            preferred_element_type=jnp.float32,
        ).astype(jnp.bfloat16)
        total = part.astype(jnp.float32) if total is None else total + part.astype(jnp.float32)
    return total


def per_device(tokens, routes, route_weight, w_gate, w_up, w_down):
    tok = tokens.shape[0]
    top = routes.shape[1]
    width = tokens.shape[1]
    experts = lax.axis_size("ex")
    sharers = lax.axis_size("sh")
    n_ctx = lax.axis_size("context")
    route_count = max(5 * experts, 2 * top)
    capacity = max(2, 5 * tok * top // (2 * route_count))
    half = -(-capacity // n_ctx)
    span = n_ctx * half
    ctx = lax.axis_index("context")
    me = lax.axis_index("ex")

    def with_sibling(x):
        return jnp.concatenate([x, shift(x, "context", n_ctx, 1)], axis=0)

    wg = with_sibling(w_gate[0])
    wu = with_sibling(w_up[0])
    wd = with_sibling(w_down[0])

    other_routes = shift(routes, "context", n_ctx, 1)
    pair_routes = jnp.where(
        ctx == 0,
        jnp.concatenate([routes, other_routes], axis=0),
        jnp.concatenate([other_routes, routes], axis=0),
    )
    ids = jnp.arange(experts, dtype=jnp.int32)
    has = jnp.any(pair_routes[None, :, :] == ids[:, None, None], axis=2).astype(jnp.int32)
    count = jnp.cumsum(has, axis=1) - has
    local_has = jnp.where(ctx == 0, has, jnp.roll(has, tok, axis=1))
    local_slot = jnp.where(ctx == 0, count, jnp.roll(count, tok, axis=1))

    if experts == 2:
        position = jnp.where(ids == me, 0, 1)
        order_has = jnp.where(me == 0, local_has, local_has[::-1])
        order_slot = jnp.where(me == 0, local_slot, local_slot[::-1])
    else:
        position = ids
        order_has, order_slot = local_has, local_slot
    wanted = ctx * half + jnp.arange(half, dtype=jnp.int32)
    picker = (order_has[:, None, :] > 0) & (order_slot[:, None, :] == wanted[None, :, None])
    picker = picker.astype(jnp.bfloat16).reshape(experts * half, n_ctx * tok)
    pair_tokens = with_sibling(tokens)
    packed = jnp.dot(picker, pair_tokens, preferred_element_type=jnp.float32).astype(jnp.bfloat16)
    packed = packed.reshape(experts, half, width)

    def exchange(x, k):
        if sharers & (sharers - 1) == 0:
            return swap(x, "sh", sharers, k)
        return shift(x, "sh", sharers, k)

    def back_exchange(x, k):
        if sharers & (sharers - 1) == 0:
            return swap(x, "sh", sharers, k)
        return shift(x, "sh", sharers, -k)

    def group_partial(sent):
        order = list(range(sharers - 1, 0, -1))
        received = {k: exchange(sent, k) for k in order}
        group = [sent] + [received[k] for k in range(1, sharers)]
        rows = jnp.stack(group).reshape(-1, width)
        partial = quarter_rows(rows, wg, wu, wd, n_ctx).astype(jnp.bfloat16)
        return partial.reshape((sharers,) + sent.shape)

    def group_sum(partial, far_first=True):
        total = partial[0].astype(jnp.float32)
        order = list(range(sharers - 1, 0, -1)) if far_first else sorted(range(1, sharers), key=lambda k: k == 2)
        for k in order:
            total = total + back_exchange(partial[k], k).astype(jnp.float32)
        return total

    if experts == 2:
        local_part = group_partial(packed[0:1])
        far_part = group_partial(shift(packed[1:2], "ex", 2, 1))
        far_out = group_sum(far_part)
        back = shift(far_out.astype(RETURN_DTYPE), "ex", 2, 1).astype(jnp.float32)
        mine = jnp.concatenate([group_sum(local_part, far_first=False), back], axis=0)
    else:
        sent = lax.all_to_all(packed, "ex", split_axis=0, concat_axis=0, tiled=True)
        expert_out = group_sum(group_partial(sent)).astype(RETURN_DTYPE)
        mine = lax.all_to_all(expert_out, "ex", split_axis=0, concat_axis=0, tiled=True)
        mine = mine.astype(jnp.float32)
    theirs = shift(mine, "context", n_ctx, 1)
    slots_out = jnp.concatenate([mine, theirs], axis=0).reshape(n_ctx * experts * half, width)

    n_slots = n_ctx * experts * half
    own_has = local_has[:, :tok] > 0
    own_slot = local_slot[:, :tok]
    weight = jnp.sum(
        jnp.where(routes[None, :, :] == ids[:, None, None], route_weight[None, :, :], 0.0), axis=2
    )
    block = jnp.where(own_slot // half == ctx, 0, 1)
    layout = block * (experts * half) + position[:, None] * half + own_slot % half
    layout = jnp.where(own_has, layout, n_slots)
    own_match = (layout[:, :, None] == jnp.arange(n_slots, dtype=jnp.int32)[None, None, :]).astype(
        jnp.float32
    )
    mixing = jnp.sum(own_match * weight[:, :, None], axis=0)
    mixed = jnp.dot(
        mixing, slots_out, precision=lax.Precision.HIGH, preferred_element_type=jnp.float32
    )
    return mixed.astype(jnp.bfloat16)


def solution(mesh):
    groups, n_expert, n_ctx = mesh.devices.shape
    split = Mesh(
        mesh.devices.reshape(groups, n_expert // SHARERS, SHARERS, n_ctx),
        ("groups", "ex", "sh", "context"),
    )
    rows = P(("groups", "ex", "sh", "context"), None)
    slabs = P(("ex", "sh"), "context", None)
    return jax.shard_map(
        per_device,
        mesh=split,
        in_specs=(rows, rows, rows, slabs, slabs, slabs),
        out_specs=rows,
        check_vma=False,
    )
```

```python
import jax
import jax.numpy as jnp
from jax import lax
from jax.sharding import Mesh
from jax.sharding import PartitionSpec as P

SHARERS = 4
RETURN_DTYPE = jnp.bfloat16


def shift(x, axis, size, k):
    return lax.ppermute(x, axis, [(i, (i + k) % size) for i in range(size)])


def swap(x, axis, size, k):
    return lax.ppermute(x, axis, [(i, i ^ k) for i in range(size)])


def quarter_rows(rows, w_gate, w_up, w_down, n_ctx):
    dims = (((1,), (1,)), ((), ()))
    gate = lax.dot_general(rows, w_gate, dims, preferred_element_type=jnp.float32)
    up = lax.dot_general(rows, w_up, dims, preferred_element_type=jnp.float32)
    hidden = (jax.nn.silu(gate) * up).astype(jnp.bfloat16)
    slab = w_down.shape[0] // n_ctx
    total = None
    for c in range(n_ctx):
        part = jnp.dot(
            hidden[:, c * slab : (c + 1) * slab],
            w_down[c * slab : (c + 1) * slab],
            preferred_element_type=jnp.float32,
        ).astype(jnp.bfloat16)
        total = part.astype(jnp.float32) if total is None else total + part.astype(jnp.float32)
    return total


def per_device(tokens, routes, route_weight, w_gate, w_up, w_down):
    tok = tokens.shape[0]
    top = routes.shape[1]
    width = tokens.shape[1]
    experts = lax.axis_size("ex")
    sharers = lax.axis_size("sh")
    n_ctx = lax.axis_size("context")
    route_count = max(5 * experts, 2 * top)
    capacity = max(2, 5 * tok * top // (2 * route_count))
    half = -(-capacity // n_ctx)
    span = n_ctx * half
    ctx = lax.axis_index("context")
    me = lax.axis_index("ex")

    def with_sibling(x):
        return jnp.concatenate([x, shift(x, "context", n_ctx, 1)], axis=0)

    wg = with_sibling(w_gate[0])
    wu = with_sibling(w_up[0])
    wd = with_sibling(w_down[0])

    other_routes = shift(routes, "context", n_ctx, 1)
    pair_routes = jnp.where(
        ctx == 0,
        jnp.concatenate([routes, other_routes], axis=0),
        jnp.concatenate([other_routes, routes], axis=0),
    )
    ids = jnp.arange(experts, dtype=jnp.int32)
    has = jnp.any(pair_routes[None, :, :] == ids[:, None, None], axis=2).astype(jnp.int32)
    count = jnp.cumsum(has, axis=1) - has
    local_has = jnp.where(ctx == 0, has, jnp.roll(has, tok, axis=1))
    local_slot = jnp.where(ctx == 0, count, jnp.roll(count, tok, axis=1))

    if experts == 2:
        position = jnp.where(ids == me, 0, 1)
        order_has = jnp.where(me == 0, local_has, local_has[::-1])
        order_slot = jnp.where(me == 0, local_slot, local_slot[::-1])
    else:
        position = ids
        order_has, order_slot = local_has, local_slot
    wanted = ctx * half + jnp.arange(half, dtype=jnp.int32)
    picker = (order_has[:, None, :] > 0) & (order_slot[:, None, :] == wanted[None, :, None])
    picker = picker.astype(jnp.bfloat16).reshape(experts * half, n_ctx * tok)
    pair_tokens = with_sibling(tokens)
    packed = jnp.dot(picker, pair_tokens, preferred_element_type=jnp.float32).astype(jnp.bfloat16)
    packed = packed.reshape(experts, half, width)

    def exchange(x, k):
        if sharers & (sharers - 1) == 0:
            return swap(x, "sh", sharers, k)
        return shift(x, "sh", sharers, k)

    def back_exchange(x, k):
        if sharers & (sharers - 1) == 0:
            return swap(x, "sh", sharers, k)
        return shift(x, "sh", sharers, -k)

    def group_partial(sent):
        order = list(range(sharers - 1, 0, -1))
        received = {k: exchange(sent, k) for k in order}
        group = [sent] + [received[k] for k in range(1, sharers)]
        rows = jnp.stack(group).reshape(-1, width)
        partial = quarter_rows(rows, wg, wu, wd, n_ctx).astype(jnp.bfloat16)
        return partial.reshape((sharers,) + sent.shape)

    def group_sum(partial, far_first=True):
        total = partial[0].astype(jnp.float32)
        for k in sorted(range(1, sharers), key=lambda k: (k == 2, -k)) if far_first else range(1, sharers):
            total = total + back_exchange(partial[k], k).astype(jnp.float32)
        return total

    if experts == 2:
        local_part = group_partial(packed[0:1])
        far_part = group_partial(shift(packed[1:2], "ex", 2, 1))
        far_out = group_sum(far_part)
        back = shift(far_out.astype(RETURN_DTYPE), "ex", 2, 1).astype(jnp.float32)
        mine = jnp.concatenate([group_sum(local_part, far_first=False), back], axis=0)
    else:
        sent = lax.all_to_all(packed, "ex", split_axis=0, concat_axis=0, tiled=True)
        expert_out = group_sum(group_partial(sent)).astype(RETURN_DTYPE)
        mine = lax.all_to_all(expert_out, "ex", split_axis=0, concat_axis=0, tiled=True)
        mine = mine.astype(jnp.float32)
    theirs = shift(mine, "context", n_ctx, 1)
    slots_out = jnp.concatenate([mine, theirs], axis=0).reshape(n_ctx * experts * half, width)

    n_slots = n_ctx * experts * half
    own_has = local_has[:, :tok] > 0
    own_slot = local_slot[:, :tok]
    weight = jnp.sum(
        jnp.where(routes[None, :, :] == ids[:, None, None], route_weight[None, :, :], 0.0), axis=2
    )
    block = jnp.where(own_slot // half == ctx, 0, 1)
    layout = block * (experts * half) + position[:, None] * half + own_slot % half
    layout = jnp.where(own_has, layout, n_slots)
    own_match = (layout[:, :, None] == jnp.arange(n_slots, dtype=jnp.int32)[None, None, :]).astype(
        jnp.float32
    )
    mixing = jnp.sum(own_match * weight[:, :, None], axis=0)
    mixed = jnp.dot(
        mixing, slots_out, precision=lax.Precision.HIGH, preferred_element_type=jnp.float32
    )
    return mixed.astype(jnp.bfloat16)


def solution(mesh):
    groups, n_expert, n_ctx = mesh.devices.shape
    split = Mesh(
        mesh.devices.reshape(groups, n_expert // SHARERS, SHARERS, n_ctx),
        ("groups", "ex", "sh", "context"),
    )
    rows = P(("groups", "ex", "sh", "context"), None)
    slabs = P(("ex", "sh"), "context", None)
    return jax.shard_map(
        per_device,
        mesh=split,
        in_specs=(rows, rows, rows, slabs, slabs, slabs),
        out_specs=rows,
        check_vma=False,
    )
```
